32 devices in a mesh: rep: 4 (over z), tp: 8 (over y, x, core).
Axes of the slice: x: 2, y: 2, z: 4, core: 2. Of those that a mesh axis runs over, the one named last changes fastest.
Arguments:
- activations: bfloat16 [6144, 1024], P(('rep', 'tp')), may hold values from -6 to 6
- out_grads: bfloat16 [6144, 3072], P('rep', 'tp'), may hold values from -0.15625 to 0.15625
- error_state: bfloat16 [4, 1024, 3072], P('rep', None, 'tp'), may hold values from -4 to 4
- q_start: float32 [3072, 32], P('tp'), may hold values from -6 to 6
- qkv_master: float32 [1024, 3072], P('rep', 'tp'), may hold values from -3 to 3
- qkv_moment: float32 [1024, 3072], P('rep', 'tp'), may hold values from -0.75 to 0.75
- word_grads: bfloat16 [6144, 1024], P('rep', 'tp'), may hold values from -6 to 6
- token_ids: int32 [6144], P('rep'), may hold values from 0 to 1599, as said below
- owner_map: int32 [1600], replicated, may hold values from 0 to 1599, as said below
- word_master: float32 [1600, 1024], P('rep', 'tp'), may hold values from -6 to 6
Outputs:
- error_new: bfloat16 [4, 1024, 3072], P('rep', None, 'tp')
- q_factor: float32 [3072, 32], P('tp')
- moment_new: float32 [1024, 3072], P('rep', 'tp')
- master_new: float32 [1024, 3072], P('rep', 'tp')
- weight_bf16: bfloat16 [1024, 3072], P(None, 'tp')
- word_new: float32 [1600, 1024], P('rep', 'tp')
The draws below stay inside these ranges and needn't reach their ends.
Inputs may be any that keep to these rules, and one draw needn't show every extreme that they name: A permutation of the rows: word w is stored in row owner_map[w] of word_master, whose owner is that row divided by 400. `token_ids`: the 1536 tokens of one replica name words of one owner at most 768 times; in every replica some owner is named exactly 768 times.
All inputs are finite; a program needn't handle non-finite values.
Results may differ from the reference program's by a relative error of at most 0.001.
Values may be sent and summed in bfloat16 or wider, within the bound.
No kernel may reach another device: no remote copies, remote signals or barrier semaphores. Data moves between devices by JAX's collectives and lax.ppermute only.
A program may use at most 64 MiB of HBM per device.

```python
import jax
import jax.numpy as jnp
from jax import lax

D = 1024
QKV = 3072
RANK = 32
ROUNDS = 2
TOK_REP = 1536
TOKENS = 6144
ROWS_DEV = 400
VOCAB = 1600
CAP = 768
N_REP = 4


def row_order(key):
    return jax.random.permutation(jax.random.fold_in(key, 7), VOCAB).astype(jnp.int32)


def draw_owner_map(key, part):
    return row_order(key)


def draw_token_ids(key, part):
    placement_order = row_order(key)
    inverse = jnp.zeros((VOCAB,), jnp.int32).at[placement_order].set(jnp.arange(VOCAB, dtype=jnp.int32))

    def replica_positions(replica):
        base_key = jax.random.fold_in(jax.random.fold_in(key, 31), replica)
        subkeys = jax.random.split(base_key, 4)
        hottest = jax.random.randint(subkeys[0], (), 0, N_REP).astype(jnp.int32)
        others = (jax.random.permutation(subkeys[1], (N_REP - 1) * CAP)[:TOK_REP - CAP] // CAP).astype(jnp.int32)
        others = others + (others >= hottest).astype(jnp.int32)
        owners = jnp.concatenate([jnp.full((CAP,), hottest, jnp.int32), others])
        within = jax.random.randint(subkeys[2], (TOK_REP,), 0, ROWS_DEV).astype(jnp.int32)
        placed = owners * ROWS_DEV + within
        return placed[jax.random.permutation(subkeys[3], TOK_REP)]
    positions = jax.vmap(replica_positions)(jnp.arange(N_REP, dtype=jnp.int32))
    return inverse[positions.reshape(-1)]


def level_of(own_key, dims, pieces, least, top_value):
    gain = 1.0
    for position, parts in pieces:
        steps = jax.random.uniform(jax.random.fold_in(jax.random.fold_in(own_key, 6), position), (parts,), jnp.float32, least / len(pieces), top_value / len(pieces))
        gain = gain * jnp.repeat(jnp.exp(steps), dims[position] // parts).reshape((-1,) + (1,) * (len(dims) - 1 - position))
    return gain


def bell_draw(stream_key, shape, width, most, cuts=(), kind=jnp.bfloat16):
    entries = jax.random.normal(stream_key, shape, jnp.float32) * width
    if len(cuts) > 0:
        entries = level_of(stream_key, shape, cuts, -0.22, 0.18) * entries
    return jnp.clip(entries, min=-most, max=most).astype(kind)


def setup_inputs(seed: int = 0) -> dict:
    keys = jax.random.split(jax.random.key(seed), 11)
    activations = bell_draw(keys[0], (TOKENS, D), 1.0, 6.0, ((0, 32),))
    out_grads = bell_draw(keys[1], (TOKENS, QKV), TOK_REP ** -0.5, 0.15625, ((0, 4), (1, 8)))
    error_state = bell_draw(keys[2], (N_REP, D, QKV), 0.5, 4.0, ((0, 4), (2, 8)))
    q_start = bell_draw(keys[3], (QKV, RANK), 1.0, 6.0, ((0, 8),), jnp.float32)
    qkv_master = bell_draw(keys[4], (D, QKV), 0.2, 3.0, ((0, 4), (1, 8)), jnp.float32)
    qkv_moment = bell_draw(keys[5], (D, QKV), 0.05, 0.75, ((0, 4), (1, 8)), jnp.float32)
    word_grads = bell_draw(keys[6], (TOKENS, D), 1.0, 6.0, ((0, 4), (1, 8)))
    token_ids = draw_token_ids(jax.random.fold_in(keys[10], 71), 0)
    owner_map = draw_owner_map(jax.random.fold_in(keys[10], 71), 0)
    word_master = bell_draw(keys[9], (VOCAB, D), 1.0, 6.0, ((0, 4), (1, 8)), jnp.float32)
    return {"activations": activations, "out_grads": out_grads, "error_state": error_state, "q_start": q_start, "qkv_master": qkv_master, "qkv_moment": qkv_moment, "word_grads": word_grads, "token_ids": token_ids, "owner_map": owner_map, "word_master": word_master}


MOMENTUM = 0.9
LEARNING_RATE = 4.0
EMBED_RATE = 0.5

def orthonormal(left_basis):
    highest = lax.Precision.HIGHEST
    gram_matrix = jnp.dot(left_basis.T, left_basis, precision=highest)
    factor_low = jnp.linalg.cholesky(gram_matrix)
    return jax.scipy.linalg.solve_triangular(factor_low, left_basis.T, lower=True).T

def reference(activations, out_grads, error_state, q_start, qkv_master, qkv_moment, word_grads, token_ids, owner_map, word_master):
    highest = lax.Precision.HIGHEST

    def replica_matrix(replica):
        first_row = (replica * TOK_REP).astype(jnp.int32)
        inputs = lax.dynamic_slice_in_dim(activations, first_row, TOK_REP, 0)
        outputs = lax.dynamic_slice_in_dim(out_grads, first_row, TOK_REP, 0)
        product = lax.dot_general(inputs.astype(jnp.float32), outputs.astype(jnp.float32), (((0,), (0,)), ((), ())), preferred_element_type=jnp.float32)
        return product + error_state[replica].astype(jnp.float32)
    combined = lax.map(replica_matrix, jnp.arange(N_REP, dtype=jnp.int32))
    right_basis = q_start
    left_basis = None
    for round_index in range(ROUNDS):
        left_basis = jnp.einsum('rdq,qk->dk', combined, right_basis, precision=highest) / N_REP
        left_basis = orthonormal(left_basis)
        right_basis = jnp.einsum('rdq,dk->qk', combined, left_basis, precision=highest) / N_REP
    approx = jnp.dot(left_basis, right_basis.T, precision=highest)
    error_new = (combined - approx[None]).astype(jnp.bfloat16)
    moment_new = MOMENTUM * qkv_moment + approx
    master_new = qkv_master - LEARNING_RATE * moment_new
    weight_bf16 = master_new.astype(jnp.bfloat16)
    stored = owner_map[token_ids]
    row_grad = jax.ops.segment_sum(word_grads.astype(jnp.float32), stored, num_segments=VOCAB)
    word_new = word_master - EMBED_RATE * row_grad
    return (error_new, right_basis, moment_new, master_new, weight_bf16, word_new)
```

```python
import jax
import jax.numpy as jnp
from jax import lax
from jax.sharding import PartitionSpec as P

ROUNDS = 2


MOMENTUM = 0.9
LEARNING_RATE = 4.0
EMBED_RATE = 0.5


def tree_sum(value, axes):
    if isinstance(axes, str):
        axes = (axes,)
    count = 1
    for axis in axes:
        count *= lax.axis_size(axis)
    if count & (count - 1):
        return lax.psum(value, axes)
    stride = 1
    while stride < count:
        pairs = [(i, i ^ stride) for i in range(count)]
        value = value + lax.ppermute(value, axes, pairs)
        stride *= 2
    return value


def orthonormal(left_basis, gram_matrix):
    factor_low = jnp.linalg.cholesky(gram_matrix)
    return jax.scipy.linalg.solve_triangular(factor_low, left_basis.T, lower=True).T


def word_update(word_grads, token_ids, owner_map, word_master):
    replicas = lax.axis_size("rep")
    per_owner = word_master.shape[0]
    capacity = 2 * token_ids.shape[0] // replicas
    targets = owner_map[token_ids]
    owners = targets // per_owner
    row_slot = targets % per_owner
    matches = (owners[:, None] == jnp.arange(replicas, dtype=jnp.int32)[None, :]).astype(jnp.int32)
    places = jnp.sum(jnp.cumsum(matches, axis=0) * matches, axis=1) - 1
    outgoing = (
        jnp.zeros((replicas, capacity, word_grads.shape[1]), jnp.bfloat16)
        .at[owners, places]
        .set(word_grads)
    )
    labels = jnp.full((replicas, capacity), per_owner, jnp.int32).at[owners, places].set(row_slot)
    incoming, arrived = (
        lax.all_to_all(outgoing, "rep", split_axis=0, concat_axis=0, tiled=True),
        lax.all_to_all(labels, "rep", split_axis=0, concat_axis=0, tiled=True),
    )
    flat_rows = incoming.reshape(-1, incoming.shape[2])
    selector = (
        arrived.reshape(-1)[:, None] == jnp.arange(per_owner, dtype=jnp.int32)[None, :]
    ).astype(jnp.bfloat16)
    row_grad = lax.dot_general(
        selector, flat_rows, (((0,), (0,)), ((), ())), preferred_element_type=jnp.float32
    )
    return word_master - EMBED_RATE * row_grad


def shards(
    activations,
    out_grads,
    error_state,
    q_start,
    qkv_master,
    qkv_moment,
    word_grads,
    token_ids,
    owner_map,
    word_master,
):
    highest = lax.Precision.HIGHEST
    replicas = lax.axis_size("rep")
    word_new = None
    product = lax.dot_general(
        lax.all_gather(activations, "tp", axis=0, tiled=True),
        out_grads,
        (((0,), (0,)), ((), ())),
        preferred_element_type=jnp.float32,
    )
    combined = product + error_state[0].astype(jnp.float32)
    right_basis = q_start
    left_basis = None
    for round_index in range(ROUNDS):
        partial_left = jnp.dot(combined, right_basis, precision=highest)
        left_basis = tree_sum(partial_left, ("rep", "tp")) / replicas
        gram_matrix = jnp.dot(left_basis.T, left_basis, precision=highest)
        left_basis = orthonormal(left_basis, gram_matrix)
        partial_right = lax.dot_general(
            combined, left_basis, (((0,), (0,)), ((), ())), precision=highest
        )
        right_basis = tree_sum(partial_right, "rep") / replicas
    approx = jnp.dot(left_basis, right_basis.T, precision=highest)
    error_new = (combined - approx).astype(jnp.bfloat16)[None]
    owned_rows = qkv_master.shape[0]
    update_rows = lax.dynamic_slice_in_dim(
        approx, lax.axis_index("rep") * owned_rows, owned_rows, 0
    )
    moment_new = MOMENTUM * qkv_moment + update_rows
    master_new = qkv_master - LEARNING_RATE * moment_new
    weight_bf16 = lax.all_gather(master_new.astype(jnp.bfloat16), "rep", axis=0, tiled=True)
    word_new = word_update(word_grads, token_ids, owner_map, word_master)
    return (error_new, right_basis, moment_new, master_new, weight_bf16, word_new)


def solution(mesh):
    in_specs = (
        P(("rep", "tp"), None),
        P("rep", "tp"),
        P("rep", None, "tp"),
        P("tp", None),
        P("rep", "tp"),
        P("rep", "tp"),
        P("rep", "tp"),
        P("rep"),
        P(),
        P("rep", "tp"),
    )
    out_specs = (
        P("rep", None, "tp"),
        P("tp", None),
        P("rep", "tp"),
        P("rep", "tp"),
        P(None, "tp"),
        P("rep", "tp"),
    )
    return jax.shard_map(shards, mesh=mesh, in_specs=in_specs, out_specs=out_specs, check_vma=False)
```

```python
import jax
import jax.numpy as jnp
from jax import lax
from jax.sharding import PartitionSpec as P

ROUNDS = 2


MOMENTUM = 0.9
LEARNING_RATE = 4.0
EMBED_RATE = 0.5


def tree_sum(value, axes):
    if isinstance(axes, str):
        axes = (axes,)
    count = 1
    for axis in axes:
        count *= lax.axis_size(axis)
    if count & (count - 1):
        return lax.psum(value, axes)
    stride = 1
    while stride < count:
        pairs = [(i, i ^ stride) for i in range(count)]
        value = value + lax.ppermute(value, axes, pairs)
        stride *= 2
    return value


def gather_rows(block, axis):
    count = lax.axis_size(axis)
    if count != 8 or block.shape[0] % 2:
        return lax.all_gather(block, axis, axis=0, tiled=True)
    me = lax.axis_index(axis)

    def exchange(value, stride):
        return lax.ppermute(value, axis, [(i, i ^ stride) for i in range(count)])

    from_x = exchange(block, 2)
    from_y = exchange(block, 4)
    half = block.shape[0] // 2
    diagonal = jnp.concatenate(
        [exchange(from_y[:half], 2), exchange(from_x[half:], 4)], axis=0
    )
    other = exchange(jnp.stack([block, from_x, from_y, diagonal]), 1)
    pieces = {0: block, 2: from_x, 4: from_y, 6: diagonal}
    for index, offset in enumerate((1, 3, 5, 7)):
        pieces[offset] = other[index]
    rows = block.shape[0]
    gathered = jnp.zeros((count * rows,) + block.shape[1:], block.dtype)
    for offset, piece in pieces.items():
        gathered = lax.dynamic_update_slice_in_dim(gathered, piece, (me ^ offset) * rows, 0)
    return gathered


def orthonormal(left_basis, gram_matrix):
    factor_low = jnp.linalg.cholesky(gram_matrix)
    return jax.scipy.linalg.solve_triangular(factor_low, left_basis.T, lower=True).T


def word_update(word_grads, token_ids, owner_map, word_master):
    replicas = lax.axis_size("rep")
    per_owner = word_master.shape[0]
    capacity = 2 * token_ids.shape[0] // replicas
    targets = owner_map[token_ids]
    owners = targets // per_owner
    row_slot = targets % per_owner
    matches = (owners[:, None] == jnp.arange(replicas, dtype=jnp.int32)[None, :]).astype(jnp.int32)
    places = jnp.sum(jnp.cumsum(matches, axis=0) * matches, axis=1) - 1
    outgoing = (
        jnp.zeros((replicas, capacity, word_grads.shape[1]), jnp.bfloat16)
        .at[owners, places]
        .set(word_grads)
    )
    labels = jnp.full((replicas, capacity), per_owner, jnp.int32).at[owners, places].set(row_slot)
    incoming, arrived = (
        lax.all_to_all(outgoing, "rep", split_axis=0, concat_axis=0, tiled=True),
        lax.all_to_all(labels, "rep", split_axis=0, concat_axis=0, tiled=True),
    )
    flat_rows = incoming.reshape(-1, incoming.shape[2])
    selector = (
        arrived.reshape(-1)[:, None] == jnp.arange(per_owner, dtype=jnp.int32)[None, :]
    ).astype(jnp.bfloat16)
    row_grad = lax.dot_general(
        selector, flat_rows, (((0,), (0,)), ((), ())), preferred_element_type=jnp.float32
    )
    return word_master - EMBED_RATE * row_grad


def shards(
    activations,
    out_grads,
    error_state,
    q_start,
    qkv_master,
    qkv_moment,
    word_grads,
    token_ids,
    owner_map,
    word_master,
):
    highest = lax.Precision.HIGHEST
    replicas = lax.axis_size("rep")
    word_new = None
    product = lax.dot_general(
        gather_rows(activations, "tp"),
        out_grads,
        (((0,), (0,)), ((), ())),
        preferred_element_type=jnp.float32,
    )
    combined = product + error_state[0].astype(jnp.float32)
    right_basis = q_start
    left_basis = None
    for round_index in range(ROUNDS):
        partial_left = jnp.dot(combined, right_basis, precision=highest)
        left_basis = tree_sum(partial_left, ("rep", "tp")) / replicas
        gram_matrix = jnp.dot(left_basis.T, left_basis, precision=highest)
        left_basis = orthonormal(left_basis, gram_matrix)
        partial_right = lax.dot_general(
            combined, left_basis, (((0,), (0,)), ((), ())), precision=highest
        )
        right_basis = tree_sum(partial_right, "rep") / replicas
    approx = jnp.dot(left_basis, right_basis.T, precision=highest)
    error_new = (combined - approx).astype(jnp.bfloat16)[None]
    owned_rows = qkv_master.shape[0]
    update_rows = lax.dynamic_slice_in_dim(
        approx, lax.axis_index("rep") * owned_rows, owned_rows, 0
    )
    moment_new = MOMENTUM * qkv_moment + update_rows
    master_new = qkv_master - LEARNING_RATE * moment_new
    weight_bf16 = lax.all_gather(master_new.astype(jnp.bfloat16), "rep", axis=0, tiled=True)
    word_new = word_update(word_grads, token_ids, owner_map, word_master)
    return (error_new, right_basis, moment_new, master_new, weight_bf16, word_new)


def solution(mesh):
    in_specs = (
        P(("rep", "tp"), None),
        P("rep", "tp"),
        P("rep", None, "tp"),
        P("tp", None),
        P("rep", "tp"),
        P("rep", "tp"),
        P("rep", "tp"),
        P("rep"),
        P(),
        P("rep", "tp"),
    )
    out_specs = (
        P("rep", None, "tp"),
        P("tp", None),
        P("rep", "tp"),
        P("rep", "tp"),
        P(None, "tp"),
        P("rep", "tp"),
    )
    return jax.shard_map(shards, mesh=mesh, in_specs=in_specs, out_specs=out_specs, check_vma=False)
```

```python
import jax
import jax.numpy as jnp
from jax import lax
from jax.sharding import PartitionSpec as P

ROUNDS = 2


MOMENTUM = 0.9
LEARNING_RATE = 4.0
EMBED_RATE = 0.5


def tree_sum(value, axes):
    if isinstance(axes, str):
        axes = (axes,)
    count = 1
    for axis in axes:
        count *= lax.axis_size(axis)
    if count & (count - 1):
        return lax.psum(value, axes)
    stride = 1
    while stride < count:
        pairs = [(i, i ^ stride) for i in range(count)]
        value = value + lax.ppermute(value, axes, pairs)
        stride *= 2
    return value


def gather_rows(block, axis):
    count = lax.axis_size(axis)
    if count != 8 or block.shape[0] % 2:
        return lax.all_gather(block, axis, axis=0, tiled=True)
    me = lax.axis_index(axis)

    def exchange(value, stride):
        return lax.ppermute(value, axis, [(i, i ^ stride) for i in range(count)])

    from_x = exchange(block, 2)
    from_y = exchange(block, 4)
    half = block.shape[0] // 2
    diagonal = jnp.concatenate(
        [exchange(from_y[:half], 2), exchange(from_x[half:], 4)], axis=0
    )
    other = exchange(jnp.stack([block, from_x, from_y, diagonal]), 1)
    pieces = {0: block, 2: from_x, 4: from_y, 6: diagonal}
    for index, offset in enumerate((1, 3, 5, 7)):
        pieces[offset] = other[index]
    rows = block.shape[0]
    gathered = jnp.zeros((count * rows,) + block.shape[1:], block.dtype)
    for offset, piece in pieces.items():
        gathered = lax.dynamic_update_slice_in_dim(gathered, piece, (me ^ offset) * rows, 0)
    return gathered


def orthonormal(left_basis, gram_matrix):
    factor_low = jnp.linalg.cholesky(gram_matrix)
    return jax.scipy.linalg.solve_triangular(factor_low, left_basis.T, lower=True).T


def word_update_dense(word_grads, token_ids, owner_map, word_master):
    replicas = lax.axis_size("rep")
    per_owner = word_master.shape[0]
    vocab = owner_map.shape[0]
    hits = token_ids[:, None] == jnp.arange(vocab, dtype=jnp.int32)[None, :]
    targets = jnp.sum(jnp.where(hits, owner_map[None, :], 0), axis=1)
    selector = (
        targets[:, None] == jnp.arange(replicas * per_owner, dtype=jnp.int32)[None, :]
    ).astype(jnp.bfloat16)
    partial = lax.dot_general(
        selector, word_grads, (((0,), (0,)), ((), ())), preferred_element_type=jnp.float32
    )
    me = lax.axis_index("rep")
    row_grad = lax.dynamic_slice_in_dim(partial, me * per_owner, per_owner, 0)
    for shift in range(1, replicas):
        block = lax.dynamic_slice_in_dim(
            partial, ((me + shift) % replicas) * per_owner, per_owner, 0
        )
        pairs = [(i, (i + shift) % replicas) for i in range(replicas)]
        row_grad = row_grad + lax.ppermute(block, "rep", pairs)
    return word_master - EMBED_RATE * row_grad


def word_update(word_grads, token_ids, owner_map, word_master):
    replicas = lax.axis_size("rep")
    if owner_map.shape[0] <= 4096 and replicas <= 8:
        return word_update_dense(word_grads, token_ids, owner_map, word_master)
    per_owner = word_master.shape[0]
    capacity = 2 * token_ids.shape[0] // replicas
    targets = owner_map[token_ids]
    owners = targets // per_owner
    row_slot = targets % per_owner
    matches = (owners[:, None] == jnp.arange(replicas, dtype=jnp.int32)[None, :]).astype(jnp.int32)
    places = jnp.sum(jnp.cumsum(matches, axis=0) * matches, axis=1) - 1
    outgoing = (
        jnp.zeros((replicas, capacity, word_grads.shape[1]), jnp.bfloat16)
        .at[owners, places]
        .set(word_grads)
    )
    labels = jnp.full((replicas, capacity), per_owner, jnp.int32).at[owners, places].set(row_slot)
    incoming, arrived = (
        lax.all_to_all(outgoing, "rep", split_axis=0, concat_axis=0, tiled=True),
        lax.all_to_all(labels, "rep", split_axis=0, concat_axis=0, tiled=True),
    )
    flat_rows = incoming.reshape(-1, incoming.shape[2])
    selector = (
        arrived.reshape(-1)[:, None] == jnp.arange(per_owner, dtype=jnp.int32)[None, :]
    ).astype(jnp.bfloat16)
    row_grad = lax.dot_general(
        selector, flat_rows, (((0,), (0,)), ((), ())), preferred_element_type=jnp.float32
    )
    return word_master - EMBED_RATE * row_grad


def shards(
    activations,
    out_grads,
    error_state,
    q_start,
    qkv_master,
    qkv_moment,
    word_grads,
    token_ids,
    owner_map,
    word_master,
):
    highest = lax.Precision.HIGHEST
    replicas = lax.axis_size("rep")
    word_new = None
    product = lax.dot_general(
        gather_rows(activations, "tp"),
        out_grads,
        (((0,), (0,)), ((), ())),
        preferred_element_type=jnp.float32,
    )
    combined = product + error_state[0].astype(jnp.float32)
    right_basis = q_start
    left_basis = None
    for round_index in range(ROUNDS):
        partial_left = jnp.dot(combined, right_basis, precision=highest)
        left_basis = tree_sum(partial_left, ("rep", "tp")) / replicas
        gram_matrix = jnp.dot(left_basis.T, left_basis, precision=highest)
        left_basis = orthonormal(left_basis, gram_matrix)
        partial_right = lax.dot_general(
            combined, left_basis, (((0,), (0,)), ((), ())), precision=highest
        )
        right_basis = tree_sum(partial_right, "rep") / replicas
    approx = jnp.dot(left_basis, right_basis.T, precision=highest)
    error_new = (combined - approx).astype(jnp.bfloat16)[None]
    owned_rows = qkv_master.shape[0]
    update_rows = lax.dynamic_slice_in_dim(
        approx, lax.axis_index("rep") * owned_rows, owned_rows, 0
    )
    moment_new = MOMENTUM * qkv_moment + update_rows
    master_new = qkv_master - LEARNING_RATE * moment_new
    weight_bf16 = lax.all_gather(master_new.astype(jnp.bfloat16), "rep", axis=0, tiled=True)
    word_new = word_update(word_grads, token_ids, owner_map, word_master)
    return (error_new, right_basis, moment_new, master_new, weight_bf16, word_new)


def solution(mesh):
    in_specs = (
        P(("rep", "tp"), None),
        P("rep", "tp"),
        P("rep", None, "tp"),
        P("tp", None),
        P("rep", "tp"),
        P("rep", "tp"),
        P("rep", "tp"),
        P("rep"),
        P(),
        P("rep", "tp"),
    )
    out_specs = (
        P("rep", None, "tp"),
        P("tp", None),
        P("rep", "tp"),
        P("rep", "tp"),
        P(None, "tp"),
        P("rep", "tp"),
    )
    return jax.shard_map(shards, mesh=mesh, in_specs=in_specs, out_specs=out_specs, check_vma=False)
```

```python
import jax
import jax.numpy as jnp
from jax import lax
from jax.sharding import PartitionSpec as P

ROUNDS = 2


MOMENTUM = 0.9
LEARNING_RATE = 4.0
EMBED_RATE = 0.5


def tree_sum(value, axes):
    if isinstance(axes, str):
        axes = (axes,)
    count = 1
    for axis in axes:
        count *= lax.axis_size(axis)
    if count & (count - 1):
        return lax.psum(value, axes)
    stride = 1
    while stride < count:
        pairs = [(i, i ^ stride) for i in range(count)]
        value = value + lax.ppermute(value, axes, pairs)
        stride *= 2
    return value


def gather_rows(block, axis):
    count = lax.axis_size(axis)
    if count != 8 or block.shape[0] % 2:
        return lax.all_gather(block, axis, axis=0, tiled=True)
    me = lax.axis_index(axis)

    def exchange(value, stride):
        return lax.ppermute(value, axis, [(i, i ^ stride) for i in range(count)])

    from_x = exchange(block, 2)
    from_y = exchange(block, 4)
    half = block.shape[0] // 2
    diagonal = jnp.concatenate(
        [exchange(from_y[:half], 2), exchange(from_x[half:], 4)], axis=0
    )
    other = exchange(jnp.stack([block, from_x, from_y, diagonal]), 1)
    pieces = {0: block, 2: from_x, 4: from_y, 6: diagonal}
    for index, offset in enumerate((1, 3, 5, 7)):
        pieces[offset] = other[index]
    rows = block.shape[0]
    gathered = jnp.zeros((count * rows,) + block.shape[1:], block.dtype)
    for offset, piece in pieces.items():
        gathered = lax.dynamic_update_slice_in_dim(gathered, piece, (me ^ offset) * rows, 0)
    return gathered


def orthonormal(left_basis, gram_matrix):
    factor_low = jnp.linalg.cholesky(gram_matrix)
    return jax.scipy.linalg.solve_triangular(factor_low, left_basis.T, lower=True).T


def word_update_dense(word_grads, token_ids, owner_map, word_master):
    replicas = lax.axis_size("rep")
    per_owner = word_master.shape[0]
    vocab = owner_map.shape[0]
    hits = token_ids[:, None] == jnp.arange(vocab, dtype=jnp.int32)[None, :]
    targets = jnp.sum(jnp.where(hits, owner_map[None, :], 0), axis=1)
    selector = (
        targets[:, None] == jnp.arange(replicas * per_owner, dtype=jnp.int32)[None, :]
    ).astype(jnp.bfloat16)
    partial = lax.dot_general(
        selector, word_grads, (((0,), (0,)), ((), ())), preferred_element_type=jnp.float32
    )
    me = lax.axis_index("rep")
    row_grad = lax.dynamic_slice_in_dim(partial, me * per_owner, per_owner, 0)
    for shift in range(1, replicas):
        block = lax.dynamic_slice_in_dim(
            partial, ((me + shift) % replicas) * per_owner, per_owner, 0
        )
        pairs = [(i, (i + shift) % replicas) for i in range(replicas)]
        row_grad = row_grad + lax.ppermute(block, "rep", pairs)
    return word_master - EMBED_RATE * row_grad


def word_update(word_grads, token_ids, owner_map, word_master):
    replicas = lax.axis_size("rep")
    if owner_map.shape[0] <= 4096 and replicas <= 8:
        return word_update_dense(word_grads, token_ids, owner_map, word_master)
    per_owner = word_master.shape[0]
    capacity = 2 * token_ids.shape[0] // replicas
    targets = owner_map[token_ids]
    owners = targets // per_owner
    row_slot = targets % per_owner
    matches = (owners[:, None] == jnp.arange(replicas, dtype=jnp.int32)[None, :]).astype(jnp.int32)
    places = jnp.sum(jnp.cumsum(matches, axis=0) * matches, axis=1) - 1
    outgoing = (
        jnp.zeros((replicas, capacity, word_grads.shape[1]), jnp.bfloat16)
        .at[owners, places]
        .set(word_grads)
    )
    labels = jnp.full((replicas, capacity), per_owner, jnp.int32).at[owners, places].set(row_slot)
    incoming, arrived = (
        lax.all_to_all(outgoing, "rep", split_axis=0, concat_axis=0, tiled=True),
        lax.all_to_all(labels, "rep", split_axis=0, concat_axis=0, tiled=True),
    )
    flat_rows = incoming.reshape(-1, incoming.shape[2])
    selector = (
        arrived.reshape(-1)[:, None] == jnp.arange(per_owner, dtype=jnp.int32)[None, :]
    ).astype(jnp.bfloat16)
    row_grad = lax.dot_general(
        selector, flat_rows, (((0,), (0,)), ((), ())), preferred_element_type=jnp.float32
    )
    return word_master - EMBED_RATE * row_grad


def shards(
    activations,
    out_grads,
    error_state,
    q_start,
    qkv_master,
    qkv_moment,
    word_grads,
    token_ids,
    owner_map,
    word_master,
):
    highest = lax.Precision.HIGHEST
    replicas = lax.axis_size("rep")
    word_new = None
    product = lax.dot_general(
        gather_rows(activations, "tp"),
        out_grads,
        (((0,), (0,)), ((), ())),
        preferred_element_type=jnp.float32,
    )
    combined = product + error_state[0].astype(jnp.float32)
    right_rows = q_start.T
    left_rows = None
    for round_index in range(ROUNDS):
        partial_left = lax.dot_general(
            right_rows, combined, (((1,), (1,)), ((), ())), precision=highest
        )
        left_rows = tree_sum(partial_left, ("rep", "tp")) / replicas
        gram_matrix = jnp.dot(left_rows, left_rows.T, precision=highest)
        factor_low = jnp.linalg.cholesky(gram_matrix)
        left_rows = jax.scipy.linalg.solve_triangular(factor_low, left_rows, lower=True)
        partial_right = jnp.dot(left_rows, combined, precision=highest)
        right_rows = tree_sum(partial_right, "rep") / replicas
    right_basis = right_rows.T
    approx = lax.dot_general(
        left_rows, right_rows, (((0,), (0,)), ((), ())), precision=highest
    )
    error_new = (combined - approx).astype(jnp.bfloat16)[None]
    owned_rows = qkv_master.shape[0]
    update_rows = lax.dynamic_slice_in_dim(
        approx, lax.axis_index("rep") * owned_rows, owned_rows, 0
    )
    moment_new = MOMENTUM * qkv_moment + update_rows
    master_new = qkv_master - LEARNING_RATE * moment_new
    weight_bf16 = lax.all_gather(master_new.astype(jnp.bfloat16), "rep", axis=0, tiled=True)
    word_new = word_update(word_grads, token_ids, owner_map, word_master)
    return (error_new, right_basis, moment_new, master_new, weight_bf16, word_new)


def solution(mesh):
    in_specs = (
        P(("rep", "tp"), None),
        P("rep", "tp"),
        P("rep", None, "tp"),
        P("tp", None),
        P("rep", "tp"),
        P("rep", "tp"),
        P("rep", "tp"),
        P("rep"),
        P(),
        P("rep", "tp"),
    )
    out_specs = (
        P("rep", None, "tp"),
        P("tp", None),
        P("rep", "tp"),
        P("rep", "tp"),
        P(None, "tp"),
        P("rep", "tp"),
    )
    return jax.shard_map(shards, mesh=mesh, in_specs=in_specs, out_specs=out_specs, check_vma=False)
```

```python
import jax
import jax.numpy as jnp
from jax import lax
from jax.sharding import PartitionSpec as P

ROUNDS = 2


MOMENTUM = 0.9
LEARNING_RATE = 4.0
EMBED_RATE = 0.5


def tree_sum(value, axes):
    if isinstance(axes, str):
        axes = (axes,)
    count = 1
    for axis in axes:
        count *= lax.axis_size(axis)
    if count & (count - 1):
        return lax.psum(value, axes)
    stride = 1
    while stride < count:
        pairs = [(i, i ^ stride) for i in range(count)]
        value = value + lax.ppermute(value, axes, pairs)
        stride *= 2
    return value


def gather_rows(block, axis):
    count = lax.axis_size(axis)
    if count != 8 or block.shape[0] % 2:
        return lax.all_gather(block, axis, axis=0, tiled=True)
    me = lax.axis_index(axis)

    def exchange(value, stride):
        return lax.ppermute(value, axis, [(i, i ^ stride) for i in range(count)])

    from_x = exchange(block, 2)
    from_y = exchange(block, 4)
    half = block.shape[0] // 2
    diagonal = jnp.concatenate(
        [exchange(from_y[:half], 2), exchange(from_x[half:], 4)], axis=0
    )
    other = exchange(jnp.stack([block, from_x, from_y, diagonal]), 1)
    pieces = {0: block, 2: from_x, 4: from_y, 6: diagonal}
    for index, offset in enumerate((1, 3, 5, 7)):
        pieces[offset] = other[index]
    rows = block.shape[0]
    gathered = jnp.zeros((count * rows,) + block.shape[1:], block.dtype)
    for offset, piece in pieces.items():
        gathered = lax.dynamic_update_slice_in_dim(gathered, piece, (me ^ offset) * rows, 0)
    return gathered


def orthonormal(left_basis, gram_matrix):
    factor_low = jnp.linalg.cholesky(gram_matrix)
    return jax.scipy.linalg.solve_triangular(factor_low, left_basis.T, lower=True).T


def word_update_dense(word_grads, token_ids, owner_map, word_master):
    replicas = lax.axis_size("rep")
    per_owner = word_master.shape[0]
    vocab = owner_map.shape[0]
    hits = token_ids[:, None] == jnp.arange(vocab, dtype=jnp.int32)[None, :]
    targets = jnp.sum(jnp.where(hits, owner_map[None, :], 0), axis=1)
    selector = (
        targets[:, None] == jnp.arange(replicas * per_owner, dtype=jnp.int32)[None, :]
    ).astype(jnp.bfloat16)
    partial = lax.dot_general(
        selector, word_grads, (((0,), (0,)), ((), ())), preferred_element_type=jnp.float32
    )
    me = lax.axis_index("rep")
    row_grad = lax.dynamic_slice_in_dim(partial, me * per_owner, per_owner, 0)
    for shift in range(1, replicas):
        block = lax.dynamic_slice_in_dim(
            partial, ((me + shift) % replicas) * per_owner, per_owner, 0
        )
        pairs = [(i, (i + shift) % replicas) for i in range(replicas)]
        row_grad = row_grad + lax.ppermute(block, "rep", pairs)
    return word_master - EMBED_RATE * row_grad


def word_update(word_grads, token_ids, owner_map, word_master):
    replicas = lax.axis_size("rep")
    if owner_map.shape[0] <= 4096 and replicas <= 8:
        return word_update_dense(word_grads, token_ids, owner_map, word_master)
    per_owner = word_master.shape[0]
    capacity = 2 * token_ids.shape[0] // replicas
    targets = owner_map[token_ids]
    owners = targets // per_owner
    row_slot = targets % per_owner
    matches = (owners[:, None] == jnp.arange(replicas, dtype=jnp.int32)[None, :]).astype(jnp.int32)
    places = jnp.sum(jnp.cumsum(matches, axis=0) * matches, axis=1) - 1
    outgoing = (
        jnp.zeros((replicas, capacity, word_grads.shape[1]), jnp.bfloat16)
        .at[owners, places]
        .set(word_grads)
    )
    labels = jnp.full((replicas, capacity), per_owner, jnp.int32).at[owners, places].set(row_slot)
    incoming, arrived = (
        lax.all_to_all(outgoing, "rep", split_axis=0, concat_axis=0, tiled=True),
        lax.all_to_all(labels, "rep", split_axis=0, concat_axis=0, tiled=True),
    )
    flat_rows = incoming.reshape(-1, incoming.shape[2])
    selector = (
        arrived.reshape(-1)[:, None] == jnp.arange(per_owner, dtype=jnp.int32)[None, :]
    ).astype(jnp.bfloat16)
    row_grad = lax.dot_general(
        selector, flat_rows, (((0,), (0,)), ((), ())), preferred_element_type=jnp.float32
    )
    return word_master - EMBED_RATE * row_grad


def shards(
    activations,
    out_grads,
    error_state,
    q_start,
    qkv_master,
    qkv_moment,
    word_grads,
    token_ids,
    owner_map,
    word_master,
):
    highest = lax.Precision.HIGHEST
    replicas = lax.axis_size("rep")
    word_new = None
    product = lax.dot_general(
        gather_rows(activations, "tp"),
        out_grads,
        (((0,), (0,)), ((), ())),
        preferred_element_type=jnp.float32,
    )
    combined = product + error_state[0].astype(jnp.float32)
    owned_rows = qkv_master.shape[0]
    if replicas <= 8:
        base_rows = qkv_master - LEARNING_RATE * (MOMENTUM * qkv_moment)
        me = lax.axis_index("rep")
        arrivals = []
        for shift in range(1, replicas):
            pairs = [(i, (i + shift) % replicas) for i in range(replicas)]
            arrivals.append(lax.ppermute(base_rows, "rep", pairs))
        arrivals, combined = lax.optimization_barrier((arrivals, combined))
        base = jnp.zeros(combined.shape, jnp.float32)
        base = lax.dynamic_update_slice_in_dim(base, base_rows, me * owned_rows, 0)
        for shift, arrived in zip(range(1, replicas), arrivals):
            source = (me + replicas - shift) % replicas
            base = lax.dynamic_update_slice_in_dim(base, arrived, source * owned_rows, 0)
    right_rows = q_start.T
    left_rows = None
    for round_index in range(ROUNDS):
        partial_left = lax.dot_general(
            right_rows, combined, (((1,), (1,)), ((), ())), precision=highest
        )
        left_rows = tree_sum(partial_left, ("rep", "tp")) / replicas
        gram_matrix = jnp.dot(left_rows, left_rows.T, precision=highest)
        factor_low = jnp.linalg.cholesky(gram_matrix)
        left_rows = jax.scipy.linalg.solve_triangular(factor_low, left_rows, lower=True)
        partial_right = jnp.dot(left_rows, combined, precision=highest)
        right_rows = tree_sum(partial_right, "rep") / replicas
    right_basis = right_rows.T
    approx = lax.dot_general(
        left_rows, right_rows, (((0,), (0,)), ((), ())), precision=highest
    )
    error_new = (combined - approx).astype(jnp.bfloat16)[None]
    update_rows = lax.dynamic_slice_in_dim(
        approx, lax.axis_index("rep") * owned_rows, owned_rows, 0
    )
    moment_new = MOMENTUM * qkv_moment + update_rows
    master_new = qkv_master - LEARNING_RATE * moment_new
    if replicas <= 8:
        weight_bf16 = (base - LEARNING_RATE * approx).astype(jnp.bfloat16)
    else:
        weight_bf16 = lax.all_gather(
            master_new.astype(jnp.bfloat16), "rep", axis=0, tiled=True
        )
    word_new = word_update(word_grads, token_ids, owner_map, word_master)
    return (error_new, right_basis, moment_new, master_new, weight_bf16, word_new)


def solution(mesh):
    in_specs = (
        P(("rep", "tp"), None),
        P("rep", "tp"),
        P("rep", None, "tp"),
        P("tp", None),
        P("rep", "tp"),
        P("rep", "tp"),
        P("rep", "tp"),
        P("rep"),
        P(),
        P("rep", "tp"),
    )
    out_specs = (
        P("rep", None, "tp"),
        P("tp", None),
        P("rep", "tp"),
        P("rep", "tp"),
        P(None, "tp"),
        P("rep", "tp"),
    )
    return jax.shard_map(shards, mesh=mesh, in_specs=in_specs, out_specs=out_specs, check_vma=False)
```

```python
import jax
import jax.numpy as jnp
from jax import lax
from jax.sharding import PartitionSpec as P

ROUNDS = 2


MOMENTUM = 0.9
LEARNING_RATE = 4.0
EMBED_RATE = 0.5


def tree_sum(value, axes):
    if isinstance(axes, str):
        axes = (axes,)
    count = 1
    for axis in axes:
        count *= lax.axis_size(axis)
    if count & (count - 1):
        return lax.psum(value, axes)

    def exchange(stride):
        return lax.ppermute(value, axes, [(i, i ^ stride) for i in range(count)])

    bits = count.bit_length() - 1
    stride = 1
    if bits % 2:
        value = value + exchange(1)
        stride = 2
    while stride < count:
        low, high = stride, 2 * stride
        value = (value + exchange(low)) + (exchange(high) + exchange(low ^ high))
        stride *= 4
    return value


def gather_rows(block, axis):
    count = lax.axis_size(axis)
    if count != 8 or block.shape[0] % 2:
        return lax.all_gather(block, axis, axis=0, tiled=True)
    me = lax.axis_index(axis)

    def exchange(value, stride):
        return lax.ppermute(value, axis, [(i, i ^ stride) for i in range(count)])

    from_x = exchange(block, 2)
    from_y = exchange(block, 4)
    half = block.shape[0] // 2
    diagonal = jnp.concatenate(
        [exchange(from_y[:half], 2), exchange(from_x[half:], 4)], axis=0
    )
    other = exchange(jnp.stack([block, from_x, from_y, diagonal]), 1)
    pieces = {0: block, 2: from_x, 4: from_y, 6: diagonal}
    for index, offset in enumerate((1, 3, 5, 7)):
        pieces[offset] = other[index]
    rows = block.shape[0]
    gathered = jnp.zeros((count * rows,) + block.shape[1:], block.dtype)
    for offset, piece in pieces.items():
        gathered = lax.dynamic_update_slice_in_dim(gathered, piece, (me ^ offset) * rows, 0)
    return gathered


def orthonormal(left_basis, gram_matrix):
    factor_low = jnp.linalg.cholesky(gram_matrix)
    return jax.scipy.linalg.solve_triangular(factor_low, left_basis.T, lower=True).T


def word_update_dense(word_grads, token_ids, owner_map, word_master):
    replicas = lax.axis_size("rep")
    per_owner = word_master.shape[0]
    vocab = owner_map.shape[0]
    hits = token_ids[:, None] == jnp.arange(vocab, dtype=jnp.int32)[None, :]
    targets = jnp.sum(jnp.where(hits, owner_map[None, :], 0), axis=1)
    selector = (
        targets[:, None] == jnp.arange(replicas * per_owner, dtype=jnp.int32)[None, :]
    ).astype(jnp.bfloat16)
    partial = lax.dot_general(
        selector, word_grads, (((0,), (0,)), ((), ())), preferred_element_type=jnp.float32
    )
    me = lax.axis_index("rep")
    row_grad = lax.dynamic_slice_in_dim(partial, me * per_owner, per_owner, 0)
    for shift in range(1, replicas):
        block = lax.dynamic_slice_in_dim(
            partial, ((me + shift) % replicas) * per_owner, per_owner, 0
        )
        pairs = [(i, (i + shift) % replicas) for i in range(replicas)]
        row_grad = row_grad + lax.ppermute(block, "rep", pairs)
    return word_master - EMBED_RATE * row_grad


def word_update(word_grads, token_ids, owner_map, word_master):
    replicas = lax.axis_size("rep")
    if owner_map.shape[0] <= 4096 and replicas <= 8:
        return word_update_dense(word_grads, token_ids, owner_map, word_master)
    per_owner = word_master.shape[0]
    capacity = 2 * token_ids.shape[0] // replicas
    targets = owner_map[token_ids]
    owners = targets // per_owner
    row_slot = targets % per_owner
    matches = (owners[:, None] == jnp.arange(replicas, dtype=jnp.int32)[None, :]).astype(jnp.int32)
    places = jnp.sum(jnp.cumsum(matches, axis=0) * matches, axis=1) - 1
    outgoing = (
        jnp.zeros((replicas, capacity, word_grads.shape[1]), jnp.bfloat16)
        .at[owners, places]
        .set(word_grads)
    )
    labels = jnp.full((replicas, capacity), per_owner, jnp.int32).at[owners, places].set(row_slot)
    incoming, arrived = (
        lax.all_to_all(outgoing, "rep", split_axis=0, concat_axis=0, tiled=True),
        lax.all_to_all(labels, "rep", split_axis=0, concat_axis=0, tiled=True),
    )
    flat_rows = incoming.reshape(-1, incoming.shape[2])
    selector = (
        arrived.reshape(-1)[:, None] == jnp.arange(per_owner, dtype=jnp.int32)[None, :]
    ).astype(jnp.bfloat16)
    row_grad = lax.dot_general(
        selector, flat_rows, (((0,), (0,)), ((), ())), preferred_element_type=jnp.float32
    )
    return word_master - EMBED_RATE * row_grad


def shards(
    activations,
    out_grads,
    error_state,
    q_start,
    qkv_master,
    qkv_moment,
    word_grads,
    token_ids,
    owner_map,
    word_master,
):
    highest = lax.Precision.HIGHEST
    replicas = lax.axis_size("rep")
    word_new = None
    product = lax.dot_general(
        gather_rows(activations, "tp"),
        out_grads,
        (((0,), (0,)), ((), ())),
        preferred_element_type=jnp.float32,
    )
    combined = product + error_state[0].astype(jnp.float32)
    right_rows = q_start.T
    left_rows = None
    for round_index in range(ROUNDS):
        partial_left = lax.dot_general(
            right_rows, combined, (((1,), (1,)), ((), ())), precision=highest
        )
        left_rows = tree_sum(partial_left, ("rep", "tp")) / replicas
        gram_matrix = jnp.dot(left_rows, left_rows.T, precision=highest)
        factor_low = jnp.linalg.cholesky(gram_matrix)
        left_rows = jax.scipy.linalg.solve_triangular(factor_low, left_rows, lower=True)
        partial_right = jnp.dot(left_rows, combined, precision=highest)
        right_rows = tree_sum(partial_right, "rep") / replicas
    right_basis = right_rows.T
    approx = lax.dot_general(
        left_rows, right_rows, (((0,), (0,)), ((), ())), precision=highest
    )
    error_new = (combined - approx).astype(jnp.bfloat16)[None]
    owned_rows = qkv_master.shape[0]
    update_rows = lax.dynamic_slice_in_dim(
        approx, lax.axis_index("rep") * owned_rows, owned_rows, 0
    )
    moment_new = MOMENTUM * qkv_moment + update_rows
    master_new = qkv_master - LEARNING_RATE * moment_new
    weight_bf16 = lax.all_gather(master_new.astype(jnp.bfloat16), "rep", axis=0, tiled=True)
    word_new = word_update(word_grads, token_ids, owner_map, word_master)
    return (error_new, right_basis, moment_new, master_new, weight_bf16, word_new)


def solution(mesh):
    in_specs = (
        P(("rep", "tp"), None),
        P("rep", "tp"),
        P("rep", None, "tp"),
        P("tp", None),
        P("rep", "tp"),
        P("rep", "tp"),
        P("rep", "tp"),
        P("rep"),
        P(),
        P("rep", "tp"),
    )
    out_specs = (
        P("rep", None, "tp"),
        P("tp", None),
        P("rep", "tp"),
        P("rep", "tp"),
        P(None, "tp"),
        P("rep", "tp"),
    )
    return jax.shard_map(shards, mesh=mesh, in_specs=in_specs, out_specs=out_specs, check_vma=False)
```

```python
import jax
import jax.numpy as jnp
from jax import lax
from jax.sharding import PartitionSpec as P

ROUNDS = 2


MOMENTUM = 0.9
LEARNING_RATE = 4.0
EMBED_RATE = 0.5


def tree_sum(value, axes):
    if isinstance(axes, str):
        axes = (axes,)
    count = 1
    for axis in axes:
        count *= lax.axis_size(axis)
    if count & (count - 1):
        return lax.psum(value, axes)
    stride = 1
    while stride < count:
        pairs = [(i, i ^ stride) for i in range(count)]
        value = value + lax.ppermute(value, axes, pairs)
        stride *= 2
    return value


def gather_rows(block, axis):
    count = lax.axis_size(axis)
    if count != 8 or block.shape[0] % 2:
        return lax.all_gather(block, axis, axis=0, tiled=True)
    me = lax.axis_index(axis)

    def exchange(value, stride):
        return lax.ppermute(value, axis, [(i, i ^ stride) for i in range(count)])

    from_x = exchange(block, 2)
    from_y = exchange(block, 4)
    half = block.shape[0] // 2
    diagonal = jnp.concatenate(
        [exchange(from_y[:half], 2), exchange(from_x[half:], 4)], axis=0
    )
    other = exchange(jnp.stack([block, from_x, from_y, diagonal]), 1)
    pieces = {0: block, 2: from_x, 4: from_y, 6: diagonal}
    for index, offset in enumerate((1, 3, 5, 7)):
        pieces[offset] = other[index]
    rows = block.shape[0]
    gathered = jnp.zeros((count * rows,) + block.shape[1:], block.dtype)
    for offset, piece in pieces.items():
        gathered = lax.dynamic_update_slice_in_dim(gathered, piece, (me ^ offset) * rows, 0)
    return gathered


def orthonormal(left_basis, gram_matrix):
    factor_low = jnp.linalg.cholesky(gram_matrix)
    return jax.scipy.linalg.solve_triangular(factor_low, left_basis.T, lower=True).T


def word_update_dense(word_grads, token_ids, owner_map, word_master):
    replicas = lax.axis_size("rep")
    per_owner = word_master.shape[0]
    vocab = owner_map.shape[0]
    hits = token_ids[:, None] == jnp.arange(vocab, dtype=jnp.int32)[None, :]
    targets = jnp.sum(jnp.where(hits, owner_map[None, :], 0), axis=1)
    selector = (
        targets[:, None] == jnp.arange(replicas * per_owner, dtype=jnp.int32)[None, :]
    ).astype(jnp.bfloat16)
    partial = lax.dot_general(
        selector, word_grads, (((0,), (0,)), ((), ())), preferred_element_type=jnp.float32
    )
    me = lax.axis_index("rep")
    row_grad = lax.dynamic_slice_in_dim(partial, me * per_owner, per_owner, 0)
    for shift in range(1, replicas):
        block = lax.dynamic_slice_in_dim(
            partial, ((me + shift) % replicas) * per_owner, per_owner, 0
        )
        pairs = [(i, (i + shift) % replicas) for i in range(replicas)]
        row_grad = row_grad + lax.ppermute(block, "rep", pairs)
    return word_master - EMBED_RATE * row_grad


def word_update(word_grads, token_ids, owner_map, word_master):
    replicas = lax.axis_size("rep")
    if owner_map.shape[0] <= 4096 and replicas <= 8:
        return word_update_dense(word_grads, token_ids, owner_map, word_master)
    per_owner = word_master.shape[0]
    capacity = 2 * token_ids.shape[0] // replicas
    targets = owner_map[token_ids]
    owners = targets // per_owner
    row_slot = targets % per_owner
    matches = (owners[:, None] == jnp.arange(replicas, dtype=jnp.int32)[None, :]).astype(jnp.int32)
    places = jnp.sum(jnp.cumsum(matches, axis=0) * matches, axis=1) - 1
    outgoing = (
        jnp.zeros((replicas, capacity, word_grads.shape[1]), jnp.bfloat16)
        .at[owners, places]
        .set(word_grads)
    )
    labels = jnp.full((replicas, capacity), per_owner, jnp.int32).at[owners, places].set(row_slot)
    incoming, arrived = (
        lax.all_to_all(outgoing, "rep", split_axis=0, concat_axis=0, tiled=True),
        lax.all_to_all(labels, "rep", split_axis=0, concat_axis=0, tiled=True),
    )
    flat_rows = incoming.reshape(-1, incoming.shape[2])
    selector = (
        arrived.reshape(-1)[:, None] == jnp.arange(per_owner, dtype=jnp.int32)[None, :]
    ).astype(jnp.bfloat16)
    row_grad = lax.dot_general(
        selector, flat_rows, (((0,), (0,)), ((), ())), preferred_element_type=jnp.float32
    )
    return word_master - EMBED_RATE * row_grad


def shards(
    activations,
    out_grads,
    error_state,
    q_start,
    qkv_master,
    qkv_moment,
    word_grads,
    token_ids,
    owner_map,
    word_master,
):
    highest = lax.Precision.HIGHEST
    replicas = lax.axis_size("rep")
    word_new = None
    product = lax.dot_general(
        gather_rows(activations, "tp"),
        out_grads,
        (((0,), (0,)), ((), ())),
        preferred_element_type=jnp.float32,
    )
    combined = product + error_state[0].astype(jnp.float32)
    word_new = word_update(word_grads, token_ids, owner_map, word_master)
    word_new, combined = lax.optimization_barrier((word_new, combined))
    right_rows = q_start.T
    left_rows = None
    for round_index in range(ROUNDS):
        partial_left = lax.dot_general(
            right_rows, combined, (((1,), (1,)), ((), ())), precision=highest
        )
        left_rows = tree_sum(partial_left, ("rep", "tp")) / replicas
        gram_matrix = jnp.dot(left_rows, left_rows.T, precision=highest)
        factor_low = jnp.linalg.cholesky(gram_matrix)
        left_rows = jax.scipy.linalg.solve_triangular(factor_low, left_rows, lower=True)
        partial_right = jnp.dot(left_rows, combined, precision=highest)
        right_rows = tree_sum(partial_right, "rep") / replicas
    right_basis = right_rows.T
    approx = lax.dot_general(
        left_rows, right_rows, (((0,), (0,)), ((), ())), precision=highest
    )
    error_new = (combined - approx).astype(jnp.bfloat16)[None]
    owned_rows = qkv_master.shape[0]
    update_rows = lax.dynamic_slice_in_dim(
        approx, lax.axis_index("rep") * owned_rows, owned_rows, 0
    )
    moment_new = MOMENTUM * qkv_moment + update_rows
    master_new = qkv_master - LEARNING_RATE * moment_new
    weight_bf16 = lax.all_gather(master_new.astype(jnp.bfloat16), "rep", axis=0, tiled=True)
    return (error_new, right_basis, moment_new, master_new, weight_bf16, word_new)


def solution(mesh):
    in_specs = (
        P(("rep", "tp"), None),
        P("rep", "tp"),
        P("rep", None, "tp"),
        P("tp", None),
        P("rep", "tp"),
        P("rep", "tp"),
        P("rep", "tp"),
        P("rep"),
        P(),
        P("rep", "tp"),
    )
    out_specs = (
        P("rep", None, "tp"),
        P("tp", None),
        P("rep", "tp"),
        P("rep", "tp"),
        P(None, "tp"),
        P("rep", "tp"),
    )
    return jax.shard_map(shards, mesh=mesh, in_specs=in_specs, out_specs=out_specs, check_vma=False)
```

```python
import jax
import jax.numpy as jnp
from jax import lax
from jax.sharding import PartitionSpec as P

ROUNDS = 2


MOMENTUM = 0.9
LEARNING_RATE = 4.0
EMBED_RATE = 0.5


def tree_sum(value, axes):
    if isinstance(axes, str):
        axes = (axes,)
    count = 1
    for axis in axes:
        count *= lax.axis_size(axis)
    if count & (count - 1):
        return lax.psum(value, axes)
    stride = 1
    while stride < count:
        pairs = [(i, i ^ stride) for i in range(count)]
        value = value + lax.ppermute(value, axes, pairs)
        stride *= 2
    return value


def replica_product(block, out_grads, axis):
    count = lax.axis_size(axis)
    if count != 8 or block.shape[0] % 2:
        gathered = lax.all_gather(block, axis, axis=0, tiled=True)
        return lax.dot_general(
            gathered, out_grads, (((0,), (0,)), ((), ())), preferred_element_type=jnp.float32
        )
    me = lax.axis_index(axis)

    def exchange(value, stride):
        return lax.ppermute(value, axis, [(i, i ^ stride) for i in range(count)])

    from_x = exchange(block, 2)
    from_y = exchange(block, 4)
    half = block.shape[0] // 2
    diagonal = jnp.concatenate(
        [exchange(from_y[:half], 2), exchange(from_x[half:], 4)], axis=0
    )
    mine = jnp.stack([block, from_x, from_y, diagonal])
    other = exchange(mine, 1)
    rows = block.shape[0]
    grads = out_grads.reshape(count, rows, out_grads.shape[1])
    even = jnp.stack([grads[me ^ offset] for offset in (0, 2, 4, 6)])
    odd = jnp.stack([grads[me ^ offset] for offset in (1, 3, 5, 7)])
    contract = (((0, 1), (0, 1)), ((), ()))
    first = lax.dot_general(mine, even, contract, preferred_element_type=jnp.float32)
    second = lax.dot_general(other, odd, contract, preferred_element_type=jnp.float32)
    return first + second


def orthonormal(left_basis, gram_matrix):
    factor_low = jnp.linalg.cholesky(gram_matrix)
    return jax.scipy.linalg.solve_triangular(factor_low, left_basis.T, lower=True).T


def word_update_dense(word_grads, token_ids, owner_map, word_master):
    replicas = lax.axis_size("rep")
    per_owner = word_master.shape[0]
    vocab = owner_map.shape[0]
    hits = token_ids[:, None] == jnp.arange(vocab, dtype=jnp.int32)[None, :]
    targets = jnp.sum(jnp.where(hits, owner_map[None, :], 0), axis=1)
    selector = (
        targets[:, None] == jnp.arange(replicas * per_owner, dtype=jnp.int32)[None, :]
    ).astype(jnp.bfloat16)
    partial = lax.dot_general(
        selector, word_grads, (((0,), (0,)), ((), ())), preferred_element_type=jnp.float32
    )
    me = lax.axis_index("rep")
    row_grad = lax.dynamic_slice_in_dim(partial, me * per_owner, per_owner, 0)
    for shift in range(1, replicas):
        block = lax.dynamic_slice_in_dim(
            partial, ((me + shift) % replicas) * per_owner, per_owner, 0
        )
        pairs = [(i, (i + shift) % replicas) for i in range(replicas)]
        row_grad = row_grad + lax.ppermute(block, "rep", pairs)
    return word_master - EMBED_RATE * row_grad


def word_update(word_grads, token_ids, owner_map, word_master):
    replicas = lax.axis_size("rep")
    if owner_map.shape[0] <= 4096 and replicas <= 8:
        return word_update_dense(word_grads, token_ids, owner_map, word_master)
    per_owner = word_master.shape[0]
    capacity = 2 * token_ids.shape[0] // replicas
    targets = owner_map[token_ids]
    owners = targets // per_owner
    row_slot = targets % per_owner
    matches = (owners[:, None] == jnp.arange(replicas, dtype=jnp.int32)[None, :]).astype(jnp.int32)
    places = jnp.sum(jnp.cumsum(matches, axis=0) * matches, axis=1) - 1
    outgoing = (
        jnp.zeros((replicas, capacity, word_grads.shape[1]), jnp.bfloat16)
        .at[owners, places]
        .set(word_grads)
    )
    labels = jnp.full((replicas, capacity), per_owner, jnp.int32).at[owners, places].set(row_slot)
    incoming, arrived = (
        lax.all_to_all(outgoing, "rep", split_axis=0, concat_axis=0, tiled=True),
        lax.all_to_all(labels, "rep", split_axis=0, concat_axis=0, tiled=True),
    )
    flat_rows = incoming.reshape(-1, incoming.shape[2])
    selector = (
        arrived.reshape(-1)[:, None] == jnp.arange(per_owner, dtype=jnp.int32)[None, :]
    ).astype(jnp.bfloat16)
    row_grad = lax.dot_general(
        selector, flat_rows, (((0,), (0,)), ((), ())), preferred_element_type=jnp.float32
    )
    return word_master - EMBED_RATE * row_grad


def shards(
    activations,
    out_grads,
    error_state,
    q_start,
    qkv_master,
    qkv_moment,
    word_grads,
    token_ids,
    owner_map,
    word_master,
):
    highest = lax.Precision.HIGHEST
    replicas = lax.axis_size("rep")
    word_new = None
    product = replica_product(activations, out_grads, "tp")
    combined = product + error_state[0].astype(jnp.float32)
    right_rows = q_start.T
    left_rows = None
    for round_index in range(ROUNDS):
        partial_left = lax.dot_general(
            right_rows, combined, (((1,), (1,)), ((), ())), precision=highest
        )
        left_rows = tree_sum(partial_left, ("rep", "tp")) / replicas
        gram_matrix = jnp.dot(left_rows, left_rows.T, precision=highest)
        factor_low = jnp.linalg.cholesky(gram_matrix)
        left_rows = jax.scipy.linalg.solve_triangular(factor_low, left_rows, lower=True)
        partial_right = jnp.dot(left_rows, combined, precision=highest)
        right_rows = tree_sum(partial_right, "rep") / replicas
    right_basis = right_rows.T
    approx = lax.dot_general(
        left_rows, right_rows, (((0,), (0,)), ((), ())), precision=highest
    )
    error_new = (combined - approx).astype(jnp.bfloat16)[None]
    owned_rows = qkv_master.shape[0]
    update_rows = lax.dynamic_slice_in_dim(
        approx, lax.axis_index("rep") * owned_rows, owned_rows, 0
    )
    moment_new = MOMENTUM * qkv_moment + update_rows
    master_new = qkv_master - LEARNING_RATE * moment_new
    weight_bf16 = lax.all_gather(master_new.astype(jnp.bfloat16), "rep", axis=0, tiled=True)
    word_new = word_update(word_grads, token_ids, owner_map, word_master)
    return (error_new, right_basis, moment_new, master_new, weight_bf16, word_new)


def solution(mesh):
    in_specs = (
        P(("rep", "tp"), None),
        P("rep", "tp"),
        P("rep", None, "tp"),
        P("tp", None),
        P("rep", "tp"),
        P("rep", "tp"),
        P("rep", "tp"),
        P("rep"),
        P(),
        P("rep", "tp"),
    )
    out_specs = (
        P("rep", None, "tp"),
        P("tp", None),
        P("rep", "tp"),
        P("rep", "tp"),
        P(None, "tp"),
        P("rep", "tp"),
    )
    return jax.shard_map(shards, mesh=mesh, in_specs=in_specs, out_specs=out_specs, check_vma=False)
```

```python
import jax
import jax.numpy as jnp
from jax import lax
from jax.sharding import PartitionSpec as P

ROUNDS = 2


MOMENTUM = 0.9
LEARNING_RATE = 4.0
EMBED_RATE = 0.5


def tree_sum(value, axes):
    if isinstance(axes, str):
        axes = (axes,)
    count = 1
    for axis in axes:
        count *= lax.axis_size(axis)
    if count & (count - 1):
        return lax.psum(value, axes)
    stride = 1
    while stride < count:
        pairs = [(i, i ^ stride) for i in range(count)]
        value = value + lax.ppermute(value, axes, pairs)
        stride *= 2
    return value


def replica_product(block, out_grads, axis):
    count = lax.axis_size(axis)
    if count != 8 or block.shape[0] % 2:
        gathered = lax.all_gather(block, axis, axis=0, tiled=True)
        return lax.dot_general(
            gathered, out_grads, (((0,), (0,)), ((), ())), preferred_element_type=jnp.float32
        )
    me = lax.axis_index(axis)

    def exchange(value, stride):
        return lax.ppermute(value, axis, [(i, i ^ stride) for i in range(count)])

    from_x = exchange(block, 2)
    from_y = exchange(block, 4)
    half = block.shape[0] // 2
    diagonal = jnp.concatenate(
        [exchange(from_y[:half], 2), exchange(from_x[half:], 4)], axis=0
    )
    mine = jnp.stack([block, from_x, from_y, diagonal])
    other = exchange(mine, 1)
    rows = block.shape[0]
    grads = out_grads.reshape(count, rows, out_grads.shape[1])
    even = jnp.stack([grads[me ^ offset] for offset in (0, 2, 4, 6)])
    odd = jnp.stack([grads[me ^ offset] for offset in (1, 3, 5, 7)])
    contract = (((0, 1), (0, 1)), ((), ()))
    first = lax.dot_general(mine, even, contract, preferred_element_type=jnp.float32)
    second = lax.dot_general(other, odd, contract, preferred_element_type=jnp.float32)
    return first + second


def orthonormal(left_basis, gram_matrix):
    factor_low = jnp.linalg.cholesky(gram_matrix)
    return jax.scipy.linalg.solve_triangular(factor_low, left_basis.T, lower=True).T


def word_update_dense(word_grads, token_ids, owner_map, word_master):
    replicas = lax.axis_size("rep")
    per_owner = word_master.shape[0]
    vocab = owner_map.shape[0]
    hits = token_ids[:, None] == jnp.arange(vocab, dtype=jnp.int32)[None, :]
    targets = jnp.sum(jnp.where(hits, owner_map[None, :], 0), axis=1)
    selector = (
        targets[:, None] == jnp.arange(replicas * per_owner, dtype=jnp.int32)[None, :]
    ).astype(jnp.bfloat16)
    partial = lax.dot_general(
        selector, word_grads, (((0,), (0,)), ((), ())), preferred_element_type=jnp.float32
    )
    me = lax.axis_index("rep")
    blocks = partial.reshape(replicas, per_owner, partial.shape[1])
    stride = 1
    while stride < replicas:
        bit = (me // stride) % 2
        paired = blocks.reshape((replicas // (2 * stride), 2) + blocks.shape[1:])
        kept = lax.dynamic_index_in_dim(paired, bit, axis=1, keepdims=False)
        sent = lax.dynamic_index_in_dim(paired, 1 - bit, axis=1, keepdims=False)
        pairs = [(i, i ^ stride) for i in range(replicas)]
        blocks = kept + lax.ppermute(sent, "rep", pairs)
        stride *= 2
    row_grad = blocks[0]
    return word_master - EMBED_RATE * row_grad


def word_update(word_grads, token_ids, owner_map, word_master):
    replicas = lax.axis_size("rep")
    if owner_map.shape[0] <= 4096 and replicas <= 8 and not replicas & (replicas - 1):
        return word_update_dense(word_grads, token_ids, owner_map, word_master)
    per_owner = word_master.shape[0]
    capacity = 2 * token_ids.shape[0] // replicas
    targets = owner_map[token_ids]
    owners = targets // per_owner
    row_slot = targets % per_owner
    matches = (owners[:, None] == jnp.arange(replicas, dtype=jnp.int32)[None, :]).astype(jnp.int32)
    places = jnp.sum(jnp.cumsum(matches, axis=0) * matches, axis=1) - 1
    outgoing = (
        jnp.zeros((replicas, capacity, word_grads.shape[1]), jnp.bfloat16)
        .at[owners, places]
        .set(word_grads)
    )
    labels = jnp.full((replicas, capacity), per_owner, jnp.int32).at[owners, places].set(row_slot)
    incoming, arrived = (
        lax.all_to_all(outgoing, "rep", split_axis=0, concat_axis=0, tiled=True),
        lax.all_to_all(labels, "rep", split_axis=0, concat_axis=0, tiled=True),
    )
    flat_rows = incoming.reshape(-1, incoming.shape[2])
    selector = (
        arrived.reshape(-1)[:, None] == jnp.arange(per_owner, dtype=jnp.int32)[None, :]
    ).astype(jnp.bfloat16)
    row_grad = lax.dot_general(
        selector, flat_rows, (((0,), (0,)), ((), ())), preferred_element_type=jnp.float32
    )
    return word_master - EMBED_RATE * row_grad


def shards(
    activations,
    out_grads,
    error_state,
    q_start,
    qkv_master,
    qkv_moment,
    word_grads,
    token_ids,
    owner_map,
    word_master,
):
    highest = lax.Precision.HIGHEST
    replicas = lax.axis_size("rep")
    word_new = None
    product = replica_product(activations, out_grads, "tp")
    combined = product + error_state[0].astype(jnp.float32)
    right_rows = q_start.T
    left_rows = None
    for round_index in range(ROUNDS):
        partial_left = lax.dot_general(
            right_rows, combined, (((1,), (1,)), ((), ())), precision=highest
        )
        left_rows = tree_sum(partial_left, ("rep", "tp")) / replicas
        gram_matrix = jnp.dot(left_rows, left_rows.T, precision=highest)
        factor_low = jnp.linalg.cholesky(gram_matrix)
        left_rows = jax.scipy.linalg.solve_triangular(factor_low, left_rows, lower=True)
        partial_right = jnp.dot(left_rows, combined, precision=highest)
        right_rows = tree_sum(partial_right, "rep") / replicas
    right_basis = right_rows.T
    approx = lax.dot_general(
        left_rows, right_rows, (((0,), (0,)), ((), ())), precision=highest
    )
    error_new = (combined - approx).astype(jnp.bfloat16)[None]
    owned_rows = qkv_master.shape[0]
    update_rows = lax.dynamic_slice_in_dim(
        approx, lax.axis_index("rep") * owned_rows, owned_rows, 0
    )
    moment_new = MOMENTUM * qkv_moment + update_rows
    master_new = qkv_master - LEARNING_RATE * moment_new
    weight_bf16 = lax.all_gather(master_new.astype(jnp.bfloat16), "rep", axis=0, tiled=True)
    word_new = word_update(word_grads, token_ids, owner_map, word_master)
    return (error_new, right_basis, moment_new, master_new, weight_bf16, word_new)


def solution(mesh):
    in_specs = (
        P(("rep", "tp"), None),
        P("rep", "tp"),
        P("rep", None, "tp"),
        P("tp", None),
        P("rep", "tp"),
        P("rep", "tp"),
        P("rep", "tp"),
        P("rep"),
        P(),
        P("rep", "tp"),
    )
    out_specs = (
        P("rep", None, "tp"),
        P("tp", None),
        P("rep", "tp"),
        P("rep", "tp"),
        P(None, "tp"),
        P("rep", "tp"),
    )
    return jax.shard_map(shards, mesh=mesh, in_specs=in_specs, out_specs=out_specs, check_vma=False)
```

```python
import jax
import jax.numpy as jnp
from jax import lax
from jax.sharding import PartitionSpec as P

ROUNDS = 2


MOMENTUM = 0.9
LEARNING_RATE = 4.0
EMBED_RATE = 0.5


def tree_sum(value, axes):
    if isinstance(axes, str):
        axes = (axes,)
    count = 1
    for axis in axes:
        count *= lax.axis_size(axis)
    if count & (count - 1):
        return lax.psum(value, axes)
    stride = 1
    while stride < count:
        pairs = [(i, i ^ stride) for i in range(count)]
        value = value + lax.ppermute(value, axes, pairs)
        stride *= 2
    return value


def replica_product(block, out_grads, axis):
    count = lax.axis_size(axis)
    if count != 8 or block.shape[0] % 2:
        gathered = lax.all_gather(block, axis, axis=0, tiled=True)
        return lax.dot_general(
            gathered, out_grads, (((0,), (0,)), ((), ())), preferred_element_type=jnp.float32
        )
    me = lax.axis_index(axis)

    def exchange(value, stride):
        return lax.ppermute(value, axis, [(i, i ^ stride) for i in range(count)])

    from_x = exchange(block, 2)
    from_y = exchange(block, 4)
    half = block.shape[0] // 2
    diagonal = jnp.concatenate(
        [exchange(from_y[:half], 2), exchange(from_x[half:], 4)], axis=0
    )
    mine = jnp.stack([block, from_x, from_y, diagonal])
    other = exchange(mine, 1)
    rows = block.shape[0]
    grads = out_grads.reshape(count, rows, out_grads.shape[1])
    even = jnp.stack([grads[me ^ offset] for offset in (0, 2, 4, 6)])
    odd = jnp.stack([grads[me ^ offset] for offset in (1, 3, 5, 7)])
    contract = (((0, 1), (0, 1)), ((), ()))
    first = lax.dot_general(mine, even, contract, preferred_element_type=jnp.float32)
    second = lax.dot_general(other, odd, contract, preferred_element_type=jnp.float32)
    return first + second


def orthonormal(left_basis, gram_matrix):
    factor_low = jnp.linalg.cholesky(gram_matrix)
    return jax.scipy.linalg.solve_triangular(factor_low, left_basis.T, lower=True).T


def word_update_dense(word_grads, token_ids, owner_map, word_master):
    replicas = lax.axis_size("rep")
    per_owner = word_master.shape[0]
    vocab = owner_map.shape[0]
    hits = token_ids[:, None] == jnp.arange(vocab, dtype=jnp.int32)[None, :]
    targets = jnp.sum(jnp.where(hits, owner_map[None, :], 0), axis=1)
    selector = (
        targets[:, None] == jnp.arange(replicas * per_owner, dtype=jnp.int32)[None, :]
    ).astype(jnp.bfloat16)
    partial = lax.dot_general(
        selector, word_grads, (((0,), (0,)), ((), ())), preferred_element_type=jnp.float32
    )
    me = lax.axis_index("rep")
    blocks = partial.reshape(replicas, per_owner, partial.shape[1])
    stride = 1
    while stride < replicas:
        bit = (me // stride) % 2
        paired = blocks.reshape((replicas // (2 * stride), 2) + blocks.shape[1:])
        kept = lax.dynamic_index_in_dim(paired, bit, axis=1, keepdims=False)
        sent = lax.dynamic_index_in_dim(paired, 1 - bit, axis=1, keepdims=False)
        pairs = [(i, i ^ stride) for i in range(replicas)]
        blocks = kept + lax.ppermute(sent, "rep", pairs)
        stride *= 2
    row_grad = blocks[0]
    return word_master - EMBED_RATE * row_grad


def word_update(word_grads, token_ids, owner_map, word_master):
    replicas = lax.axis_size("rep")
    if owner_map.shape[0] <= 4096 and replicas <= 8 and not replicas & (replicas - 1):
        return word_update_dense(word_grads, token_ids, owner_map, word_master)
    per_owner = word_master.shape[0]
    capacity = 2 * token_ids.shape[0] // replicas
    targets = owner_map[token_ids]
    owners = targets // per_owner
    row_slot = targets % per_owner
    matches = (owners[:, None] == jnp.arange(replicas, dtype=jnp.int32)[None, :]).astype(jnp.int32)
    places = jnp.sum(jnp.cumsum(matches, axis=0) * matches, axis=1) - 1
    outgoing = (
        jnp.zeros((replicas, capacity, word_grads.shape[1]), jnp.bfloat16)
        .at[owners, places]
        .set(word_grads)
    )
    labels = jnp.full((replicas, capacity), per_owner, jnp.int32).at[owners, places].set(row_slot)
    incoming, arrived = (
        lax.all_to_all(outgoing, "rep", split_axis=0, concat_axis=0, tiled=True),
        lax.all_to_all(labels, "rep", split_axis=0, concat_axis=0, tiled=True),
    )
    flat_rows = incoming.reshape(-1, incoming.shape[2])
    selector = (
        arrived.reshape(-1)[:, None] == jnp.arange(per_owner, dtype=jnp.int32)[None, :]
    ).astype(jnp.bfloat16)
    row_grad = lax.dot_general(
        selector, flat_rows, (((0,), (0,)), ((), ())), preferred_element_type=jnp.float32
    )
    return word_master - EMBED_RATE * row_grad


def shards(
    activations,
    out_grads,
    error_state,
    q_start,
    qkv_master,
    qkv_moment,
    word_grads,
    token_ids,
    owner_map,
    word_master,
):
    highest = lax.Precision.HIGHEST
    replicas = lax.axis_size("rep")
    word_new = None
    product = replica_product(activations, out_grads, "tp")
    combined = product + error_state[0].astype(jnp.float32)
    right_rows = q_start.T
    left_rows = None
    for round_index in range(ROUNDS):
        partial_left = lax.dot_general(
            right_rows, combined, (((1,), (1,)), ((), ())), precision=highest
        )
        left_rows = tree_sum(partial_left, ("rep", "tp")) / replicas
        gram_matrix = jnp.dot(left_rows, left_rows.T, precision=highest)
        factor_low = jnp.linalg.cholesky(gram_matrix)
        left_rows = jax.scipy.linalg.solve_triangular(factor_low, left_rows, lower=True)
        if round_index == 0:
            word_new = word_update(word_grads, token_ids, owner_map, word_master)
            word_new, left_rows = lax.optimization_barrier((word_new, left_rows))
        partial_right = jnp.dot(left_rows, combined, precision=highest)
        right_rows = tree_sum(partial_right, "rep") / replicas
    right_basis = right_rows.T
    approx = lax.dot_general(
        left_rows, right_rows, (((0,), (0,)), ((), ())), precision=highest
    )
    error_new = (combined - approx).astype(jnp.bfloat16)[None]
    owned_rows = qkv_master.shape[0]
    update_rows = lax.dynamic_slice_in_dim(
        approx, lax.axis_index("rep") * owned_rows, owned_rows, 0
    )
    moment_new = MOMENTUM * qkv_moment + update_rows
    master_new = qkv_master - LEARNING_RATE * moment_new
    weight_bf16 = lax.all_gather(master_new.astype(jnp.bfloat16), "rep", axis=0, tiled=True)
    return (error_new, right_basis, moment_new, master_new, weight_bf16, word_new)


def solution(mesh):
    in_specs = (
        P(("rep", "tp"), None),
        P("rep", "tp"),
        P("rep", None, "tp"),
        P("tp", None),
        P("rep", "tp"),
        P("rep", "tp"),
        P("rep", "tp"),
        P("rep"),
        P(),
        P("rep", "tp"),
    )
    out_specs = (
        P("rep", None, "tp"),
        P("tp", None),
        P("rep", "tp"),
        P("rep", "tp"),
        P(None, "tp"),
        P("rep", "tp"),
    )
    return jax.shard_map(shards, mesh=mesh, in_specs=in_specs, out_specs=out_specs, check_vma=False)
```

```python
import jax
import jax.numpy as jnp
from jax import lax
from jax.sharding import PartitionSpec as P

ROUNDS = 2


MOMENTUM = 0.9
LEARNING_RATE = 4.0
EMBED_RATE = 0.5


def tree_sum(value, axes):
    if isinstance(axes, str):
        axes = (axes,)
    count = 1
    for axis in axes:
        count *= lax.axis_size(axis)
    if count & (count - 1):
        return lax.psum(value, axes)
    stride = 1
    while stride < count:
        pairs = [(i, i ^ stride) for i in range(count)]
        value = value + lax.ppermute(value, axes, pairs)
        stride *= 2
    return value


def replica_product(block, out_grads, axis):
    count = lax.axis_size(axis)
    if count != 8 or block.shape[0] % 2:
        gathered = lax.all_gather(block, axis, axis=0, tiled=True)
        return lax.dot_general(
            gathered, out_grads, (((0,), (0,)), ((), ())), preferred_element_type=jnp.float32
        )
    me = lax.axis_index(axis)

    def exchange(value, stride):
        return lax.ppermute(value, axis, [(i, i ^ stride) for i in range(count)])

    from_x = exchange(block, 2)
    from_y = exchange(block, 4)
    half = block.shape[0] // 2
    diagonal = jnp.concatenate(
        [exchange(from_y[:half], 2), exchange(from_x[half:], 4)], axis=0
    )
    mine = jnp.stack([block, from_x, from_y, diagonal])
    other = exchange(mine, 1)
    rows = block.shape[0]
    grads = out_grads.reshape(count, rows, out_grads.shape[1])
    even = jnp.stack([grads[me ^ offset] for offset in (0, 2, 4, 6)])
    odd = jnp.stack([grads[me ^ offset] for offset in (1, 3, 5, 7)])
    contract = (((0, 1), (0, 1)), ((), ()))
    first = lax.dot_general(mine, even, contract, preferred_element_type=jnp.float32)
    second = lax.dot_general(other, odd, contract, preferred_element_type=jnp.float32)
    return first + second


def orthonormal(left_basis, gram_matrix):
    factor_low = jnp.linalg.cholesky(gram_matrix)
    return jax.scipy.linalg.solve_triangular(factor_low, left_basis.T, lower=True).T


def word_update_dense(word_grads, token_ids, owner_map, word_master):
    replicas = lax.axis_size("rep")
    per_owner = word_master.shape[0]
    vocab = owner_map.shape[0]
    hits = token_ids[:, None] == jnp.arange(vocab, dtype=jnp.int32)[None, :]
    targets = jnp.sum(jnp.where(hits, owner_map[None, :], 0), axis=1)
    selector = (
        targets[:, None] == jnp.arange(replicas * per_owner, dtype=jnp.int32)[None, :]
    ).astype(jnp.bfloat16)
    partial = lax.dot_general(
        selector, word_grads, (((0,), (0,)), ((), ())), preferred_element_type=jnp.float32
    )
    me = lax.axis_index("rep")
    blocks = partial.reshape(replicas, per_owner, partial.shape[1])
    stride = 1
    while stride < replicas:
        bit = (me // stride) % 2
        paired = blocks.reshape((replicas // (2 * stride), 2) + blocks.shape[1:])
        kept = lax.dynamic_index_in_dim(paired, bit, axis=1, keepdims=False)
        sent = lax.dynamic_index_in_dim(paired, 1 - bit, axis=1, keepdims=False)
        pairs = [(i, i ^ stride) for i in range(replicas)]
        blocks = kept + lax.ppermute(sent, "rep", pairs)
        stride *= 2
    row_grad = blocks[0]
    return word_master - EMBED_RATE * row_grad


def word_update(word_grads, token_ids, owner_map, word_master):
    replicas = lax.axis_size("rep")
    if owner_map.shape[0] <= 4096 and replicas <= 8 and not replicas & (replicas - 1):
        return word_update_dense(word_grads, token_ids, owner_map, word_master)
    per_owner = word_master.shape[0]
    capacity = 2 * token_ids.shape[0] // replicas
    targets = owner_map[token_ids]
    owners = targets // per_owner
    row_slot = targets % per_owner
    matches = (owners[:, None] == jnp.arange(replicas, dtype=jnp.int32)[None, :]).astype(jnp.int32)
    places = jnp.sum(jnp.cumsum(matches, axis=0) * matches, axis=1) - 1
    outgoing = (
        jnp.zeros((replicas, capacity, word_grads.shape[1]), jnp.bfloat16)
        .at[owners, places]
        .set(word_grads)
    )
    labels = jnp.full((replicas, capacity), per_owner, jnp.int32).at[owners, places].set(row_slot)
    incoming, arrived = (
        lax.all_to_all(outgoing, "rep", split_axis=0, concat_axis=0, tiled=True),
        lax.all_to_all(labels, "rep", split_axis=0, concat_axis=0, tiled=True),
    )
    flat_rows = incoming.reshape(-1, incoming.shape[2])
    selector = (
        arrived.reshape(-1)[:, None] == jnp.arange(per_owner, dtype=jnp.int32)[None, :]
    ).astype(jnp.bfloat16)
    row_grad = lax.dot_general(
        selector, flat_rows, (((0,), (0,)), ((), ())), preferred_element_type=jnp.float32
    )
    return word_master - EMBED_RATE * row_grad


def shards(
    activations,
    out_grads,
    error_state,
    q_start,
    qkv_master,
    qkv_moment,
    word_grads,
    token_ids,
    owner_map,
    word_master,
):
    highest = lax.Precision.HIGHEST
    high = lax.Precision.HIGH
    replicas = lax.axis_size("rep")
    word_new = None
    product = replica_product(activations, out_grads, "tp")
    combined = product + error_state[0].astype(jnp.float32)
    right_rows = q_start.T
    left_rows = None
    for round_index in range(ROUNDS):
        partial_left = lax.dot_general(
            right_rows, combined, (((1,), (1,)), ((), ())), precision=high
        )
        left_rows = tree_sum(partial_left, ("rep", "tp")) / replicas
        gram_matrix = jnp.dot(left_rows, left_rows.T, precision=highest)
        factor_low = jnp.linalg.cholesky(gram_matrix)
        left_rows = jax.scipy.linalg.solve_triangular(factor_low, left_rows, lower=True)
        partial_right = jnp.dot(left_rows, combined, precision=high)
        right_rows = tree_sum(partial_right, "rep") / replicas
    right_basis = right_rows.T
    approx = lax.dot_general(
        left_rows, right_rows, (((0,), (0,)), ((), ())), precision=high
    )
    error_new = (combined - approx).astype(jnp.bfloat16)[None]
    owned_rows = qkv_master.shape[0]
    update_rows = lax.dynamic_slice_in_dim(
        approx, lax.axis_index("rep") * owned_rows, owned_rows, 0
    )
    moment_new = MOMENTUM * qkv_moment + update_rows
    master_new = qkv_master - LEARNING_RATE * moment_new
    weight_bf16 = lax.all_gather(master_new.astype(jnp.bfloat16), "rep", axis=0, tiled=True)
    word_new = word_update(word_grads, token_ids, owner_map, word_master)
    return (error_new, right_basis, moment_new, master_new, weight_bf16, word_new)


def solution(mesh):
    in_specs = (
        P(("rep", "tp"), None),
        P("rep", "tp"),
        P("rep", None, "tp"),
        P("tp", None),
        P("rep", "tp"),
        P("rep", "tp"),
        P("rep", "tp"),
        P("rep"),
        P(),
        P("rep", "tp"),
    )
    out_specs = (
        P("rep", None, "tp"),
        P("tp", None),
        P("rep", "tp"),
        P("rep", "tp"),
        P(None, "tp"),
        P("rep", "tp"),
    )
    return jax.shard_map(shards, mesh=mesh, in_specs=in_specs, out_specs=out_specs, check_vma=False)
```

```python
import jax
import jax.numpy as jnp
from jax import lax
from jax.sharding import PartitionSpec as P

ROUNDS = 2


MOMENTUM = 0.9
LEARNING_RATE = 4.0
EMBED_RATE = 0.5


def tree_sum(value, axes):
    if isinstance(axes, str):
        axes = (axes,)
    count = 1
    for axis in axes:
        count *= lax.axis_size(axis)
    if count & (count - 1):
        return lax.psum(value, axes)
    stride = 1
    while stride < count:
        pairs = [(i, i ^ stride) for i in range(count)]
        value = value + lax.ppermute(value, axes, pairs)
        stride *= 2
    return value


def replica_product(block, out_grads, axis):
    count = lax.axis_size(axis)
    if count != 8 or block.shape[0] % 2:
        gathered = lax.all_gather(block, axis, axis=0, tiled=True)
        return lax.dot_general(
            gathered, out_grads, (((0,), (0,)), ((), ())), preferred_element_type=jnp.float32
        )
    me = lax.axis_index(axis)

    def exchange(value, stride):
        return lax.ppermute(value, axis, [(i, i ^ stride) for i in range(count)])

    from_x = exchange(block, 2)
    from_y = exchange(block, 4)
    half = block.shape[0] // 2
    diagonal = jnp.concatenate(
        [exchange(from_y[:half], 2), exchange(from_x[half:], 4)], axis=0
    )
    mine = jnp.stack([block, from_x, from_y, diagonal])
    other = exchange(mine, 1)
    rows = block.shape[0]
    grads = out_grads.reshape(count, rows, out_grads.shape[1])
    even = jnp.stack([grads[me ^ offset] for offset in (0, 2, 4, 6)])
    odd = jnp.stack([grads[me ^ offset] for offset in (1, 3, 5, 7)])
    contract = (((0, 1), (0, 1)), ((), ()))
    first = lax.dot_general(mine, even, contract, preferred_element_type=jnp.float32)
    second = lax.dot_general(other, odd, contract, preferred_element_type=jnp.float32)
    return first + second


def split_tree_sum(value, axes):
    count = 1
    for axis in axes:
        count *= lax.axis_size(axis)
    rows = value.shape[0]
    if count & (count - 1) or count < 4 or rows % 2:
        return tree_sum(value, axes)

    def exchange(piece, stride):
        return lax.ppermute(piece, axes, [(i, i ^ stride) for i in range(count)])

    half = rows // 2
    core = lax.axis_index(axes[-1]) % 2
    kept = lax.dynamic_slice_in_dim(value, core * half, half, 0)
    given = lax.dynamic_slice_in_dim(value, (1 - core) * half, half, 0)
    kept = kept + exchange(given, 1)
    stride = 2
    while stride < count:
        kept = kept + exchange(kept, stride)
        stride *= 2
    other = exchange(kept, 1)
    total = jnp.zeros(value.shape, value.dtype)
    total = lax.dynamic_update_slice_in_dim(total, kept, core * half, 0)
    return lax.dynamic_update_slice_in_dim(total, other, (1 - core) * half, 0)


def orthonormal(left_basis, gram_matrix):
    factor_low = jnp.linalg.cholesky(gram_matrix)
    return jax.scipy.linalg.solve_triangular(factor_low, left_basis.T, lower=True).T


def word_update_dense(word_grads, token_ids, owner_map, word_master):
    replicas = lax.axis_size("rep")
    per_owner = word_master.shape[0]
    vocab = owner_map.shape[0]
    hits = token_ids[:, None] == jnp.arange(vocab, dtype=jnp.int32)[None, :]
    targets = jnp.sum(jnp.where(hits, owner_map[None, :], 0), axis=1)
    selector = (
        targets[:, None] == jnp.arange(replicas * per_owner, dtype=jnp.int32)[None, :]
    ).astype(jnp.bfloat16)
    partial = lax.dot_general(
        selector, word_grads, (((0,), (0,)), ((), ())), preferred_element_type=jnp.float32
    )
    me = lax.axis_index("rep")
    blocks = partial.reshape(replicas, per_owner, partial.shape[1])
    stride = 1
    while stride < replicas:
        bit = (me // stride) % 2
        paired = blocks.reshape((replicas // (2 * stride), 2) + blocks.shape[1:])
        kept = lax.dynamic_index_in_dim(paired, bit, axis=1, keepdims=False)
        sent = lax.dynamic_index_in_dim(paired, 1 - bit, axis=1, keepdims=False)
        pairs = [(i, i ^ stride) for i in range(replicas)]
        blocks = kept + lax.ppermute(sent, "rep", pairs)
        stride *= 2
    row_grad = blocks[0]
    return word_master - EMBED_RATE * row_grad


def word_update(word_grads, token_ids, owner_map, word_master):
    replicas = lax.axis_size("rep")
    if owner_map.shape[0] <= 4096 and replicas <= 8 and not replicas & (replicas - 1):
        return word_update_dense(word_grads, token_ids, owner_map, word_master)
    per_owner = word_master.shape[0]
    capacity = 2 * token_ids.shape[0] // replicas
    targets = owner_map[token_ids]
    owners = targets // per_owner
    row_slot = targets % per_owner
    matches = (owners[:, None] == jnp.arange(replicas, dtype=jnp.int32)[None, :]).astype(jnp.int32)
    places = jnp.sum(jnp.cumsum(matches, axis=0) * matches, axis=1) - 1
    outgoing = (
        jnp.zeros((replicas, capacity, word_grads.shape[1]), jnp.bfloat16)
        .at[owners, places]
        .set(word_grads)
    )
    labels = jnp.full((replicas, capacity), per_owner, jnp.int32).at[owners, places].set(row_slot)
    incoming, arrived = (
        lax.all_to_all(outgoing, "rep", split_axis=0, concat_axis=0, tiled=True),
        lax.all_to_all(labels, "rep", split_axis=0, concat_axis=0, tiled=True),
    )
    flat_rows = incoming.reshape(-1, incoming.shape[2])
    selector = (
        arrived.reshape(-1)[:, None] == jnp.arange(per_owner, dtype=jnp.int32)[None, :]
    ).astype(jnp.bfloat16)
    row_grad = lax.dot_general(
        selector, flat_rows, (((0,), (0,)), ((), ())), preferred_element_type=jnp.float32
    )
    return word_master - EMBED_RATE * row_grad


def shards(
    activations,
    out_grads,
    error_state,
    q_start,
    qkv_master,
    qkv_moment,
    word_grads,
    token_ids,
    owner_map,
    word_master,
):
    highest = lax.Precision.HIGHEST
    high = lax.Precision.HIGH
    replicas = lax.axis_size("rep")
    word_new = None
    product = replica_product(activations, out_grads, "tp")
    combined = product + error_state[0].astype(jnp.float32)
    right_rows = q_start.T
    left_rows = None
    for round_index in range(ROUNDS):
        partial_left = lax.dot_general(
            right_rows, combined, (((1,), (1,)), ((), ())), precision=high
        )
        left_rows = split_tree_sum(partial_left, ("rep", "tp")) / replicas
        gram_matrix = jnp.dot(left_rows, left_rows.T, precision=highest)
        factor_low = jnp.linalg.cholesky(gram_matrix)
        left_rows = jax.scipy.linalg.solve_triangular(factor_low, left_rows, lower=True)
        partial_right = jnp.dot(left_rows, combined, precision=high)
        right_rows = tree_sum(partial_right, "rep") / replicas
    right_basis = right_rows.T
    approx = lax.dot_general(
        left_rows, right_rows, (((0,), (0,)), ((), ())), precision=high
    )
    error_new = (combined - approx).astype(jnp.bfloat16)[None]
    owned_rows = qkv_master.shape[0]
    update_rows = lax.dynamic_slice_in_dim(
        approx, lax.axis_index("rep") * owned_rows, owned_rows, 0
    )
    moment_new = MOMENTUM * qkv_moment + update_rows
    master_new = qkv_master - LEARNING_RATE * moment_new
    weight_bf16 = lax.all_gather(master_new.astype(jnp.bfloat16), "rep", axis=0, tiled=True)
    word_new = word_update(word_grads, token_ids, owner_map, word_master)
    return (error_new, right_basis, moment_new, master_new, weight_bf16, word_new)


def solution(mesh):
    in_specs = (
        P(("rep", "tp"), None),
        P("rep", "tp"),
        P("rep", None, "tp"),
        P("tp", None),
        P("rep", "tp"),
        P("rep", "tp"),
        P("rep", "tp"),
        P("rep"),
        P(),
        P("rep", "tp"),
    )
    out_specs = (
        P("rep", None, "tp"),
        P("tp", None),
        P("rep", "tp"),
        P("rep", "tp"),
        P(None, "tp"),
        P("rep", "tp"),
    )
    return jax.shard_map(shards, mesh=mesh, in_specs=in_specs, out_specs=out_specs, check_vma=False)
```

```python
import jax
import jax.numpy as jnp
from jax import lax
from jax.sharding import PartitionSpec as P

ROUNDS = 2


MOMENTUM = 0.9
LEARNING_RATE = 4.0
EMBED_RATE = 0.5


def tree_sum(value, axes):
    if isinstance(axes, str):
        axes = (axes,)
    count = 1
    for axis in axes:
        count *= lax.axis_size(axis)
    if count & (count - 1):
        return lax.psum(value, axes)
    stride = 1
    while stride < count:
        pairs = [(i, i ^ stride) for i in range(count)]
        value = value + lax.ppermute(value, axes, pairs)
        stride *= 2
    return value


def replica_product(block, out_grads, axis):
    count = lax.axis_size(axis)
    if count != 8 or block.shape[0] % 2:
        gathered = lax.all_gather(block, axis, axis=0, tiled=True)
        return lax.dot_general(
            gathered, out_grads, (((0,), (0,)), ((), ())), preferred_element_type=jnp.float32
        )
    me = lax.axis_index(axis)

    def exchange(value, stride):
        return lax.ppermute(value, axis, [(i, i ^ stride) for i in range(count)])

    from_x = exchange(block, 2)
    from_y = exchange(block, 4)
    half = block.shape[0] // 2
    diagonal = jnp.concatenate(
        [exchange(from_y[:half], 2), exchange(from_x[half:], 4)], axis=0
    )
    mine = jnp.stack([block, from_x, from_y, diagonal])
    other = exchange(mine, 1)
    rows = block.shape[0]
    grads = out_grads.reshape(count, rows, out_grads.shape[1])
    even = jnp.stack([grads[me ^ offset] for offset in (0, 2, 4, 6)])
    odd = jnp.stack([grads[me ^ offset] for offset in (1, 3, 5, 7)])
    contract = (((0, 1), (0, 1)), ((), ()))
    first = lax.dot_general(mine, even, contract, preferred_element_type=jnp.float32)
    return first, (other, odd)


def split_tree_sum(value, axes):
    count = 1
    for axis in axes:
        count *= lax.axis_size(axis)
    rows = value.shape[0]
    if count & (count - 1) or count < 4 or rows % 2:
        return tree_sum(value, axes)

    def exchange(piece, stride):
        return lax.ppermute(piece, axes, [(i, i ^ stride) for i in range(count)])

    half = rows // 2
    core = lax.axis_index(axes[-1]) % 2
    kept = lax.dynamic_slice_in_dim(value, core * half, half, 0)
    given = lax.dynamic_slice_in_dim(value, (1 - core) * half, half, 0)
    kept = kept + exchange(given, 1)
    stride = 2
    while stride < count:
        kept = kept + exchange(kept, stride)
        stride *= 2
    other = exchange(kept, 1)
    total = jnp.zeros(value.shape, value.dtype)
    total = lax.dynamic_update_slice_in_dim(total, kept, core * half, 0)
    return lax.dynamic_update_slice_in_dim(total, other, (1 - core) * half, 0)


def orthonormal(left_basis, gram_matrix):
    factor_low = jnp.linalg.cholesky(gram_matrix)
    return jax.scipy.linalg.solve_triangular(factor_low, left_basis.T, lower=True).T


def word_update_dense(word_grads, token_ids, owner_map, word_master):
    replicas = lax.axis_size("rep")
    per_owner = word_master.shape[0]
    vocab = owner_map.shape[0]
    hits = token_ids[:, None] == jnp.arange(vocab, dtype=jnp.int32)[None, :]
    targets = jnp.sum(jnp.where(hits, owner_map[None, :], 0), axis=1)
    selector = (
        targets[:, None] == jnp.arange(replicas * per_owner, dtype=jnp.int32)[None, :]
    ).astype(jnp.bfloat16)
    partial = lax.dot_general(
        selector, word_grads, (((0,), (0,)), ((), ())), preferred_element_type=jnp.float32
    )
    me = lax.axis_index("rep")
    blocks = partial.reshape(replicas, per_owner, partial.shape[1])
    stride = 1
    while stride < replicas:
        bit = (me // stride) % 2
        paired = blocks.reshape((replicas // (2 * stride), 2) + blocks.shape[1:])
        kept = lax.dynamic_index_in_dim(paired, bit, axis=1, keepdims=False)
        sent = lax.dynamic_index_in_dim(paired, 1 - bit, axis=1, keepdims=False)
        pairs = [(i, i ^ stride) for i in range(replicas)]
        blocks = kept + lax.ppermute(sent, "rep", pairs)
        stride *= 2
    row_grad = blocks[0]
    return word_master - EMBED_RATE * row_grad


def word_update(word_grads, token_ids, owner_map, word_master):
    replicas = lax.axis_size("rep")
    if owner_map.shape[0] <= 4096 and replicas <= 8 and not replicas & (replicas - 1):
        return word_update_dense(word_grads, token_ids, owner_map, word_master)
    per_owner = word_master.shape[0]
    capacity = 2 * token_ids.shape[0] // replicas
    targets = owner_map[token_ids]
    owners = targets // per_owner
    row_slot = targets % per_owner
    matches = (owners[:, None] == jnp.arange(replicas, dtype=jnp.int32)[None, :]).astype(jnp.int32)
    places = jnp.sum(jnp.cumsum(matches, axis=0) * matches, axis=1) - 1
    outgoing = (
        jnp.zeros((replicas, capacity, word_grads.shape[1]), jnp.bfloat16)
        .at[owners, places]
        .set(word_grads)
    )
    labels = jnp.full((replicas, capacity), per_owner, jnp.int32).at[owners, places].set(row_slot)
    incoming, arrived = (
        lax.all_to_all(outgoing, "rep", split_axis=0, concat_axis=0, tiled=True),
        lax.all_to_all(labels, "rep", split_axis=0, concat_axis=0, tiled=True),
    )
    flat_rows = incoming.reshape(-1, incoming.shape[2])
    selector = (
        arrived.reshape(-1)[:, None] == jnp.arange(per_owner, dtype=jnp.int32)[None, :]
    ).astype(jnp.bfloat16)
    row_grad = lax.dot_general(
        selector, flat_rows, (((0,), (0,)), ((), ())), preferred_element_type=jnp.float32
    )
    return word_master - EMBED_RATE * row_grad


def shards(
    activations,
    out_grads,
    error_state,
    q_start,
    qkv_master,
    qkv_moment,
    word_grads,
    token_ids,
    owner_map,
    word_master,
):
    highest = lax.Precision.HIGHEST
    high = lax.Precision.HIGH
    replicas = lax.axis_size("rep")
    word_new = None
    early, late = replica_product(activations, out_grads, "tp")
    combined = early + error_state[0].astype(jnp.float32)
    right_rows = q_start.T
    left_rows = None
    for round_index in range(ROUNDS):
        partial_left = lax.dot_general(
            right_rows, combined, (((1,), (1,)), ((), ())), precision=high
        )
        if late is not None:
            other, odd = late
            partial_left, other = lax.optimization_barrier((partial_left, other))
            contract = (((0, 1), (0, 1)), ((), ()))
            second = lax.dot_general(other, odd, contract, preferred_element_type=jnp.float32)
            partial_left = partial_left + lax.dot_general(
                right_rows, second, (((1,), (1,)), ((), ())), precision=high
            )
            combined = combined + second
            late = None
        left_rows = split_tree_sum(partial_left, ("rep", "tp")) / replicas
        gram_matrix = jnp.dot(left_rows, left_rows.T, precision=highest)
        factor_low = jnp.linalg.cholesky(gram_matrix)
        left_rows = jax.scipy.linalg.solve_triangular(factor_low, left_rows, lower=True)
        partial_right = jnp.dot(left_rows, combined, precision=high)
        right_rows = tree_sum(partial_right, "rep") / replicas
    right_basis = right_rows.T
    approx = lax.dot_general(
        left_rows, right_rows, (((0,), (0,)), ((), ())), precision=high
    )
    error_new = (combined - approx).astype(jnp.bfloat16)[None]
    owned_rows = qkv_master.shape[0]
    update_rows = lax.dynamic_slice_in_dim(
        approx, lax.axis_index("rep") * owned_rows, owned_rows, 0
    )
    moment_new = MOMENTUM * qkv_moment + update_rows
    master_new = qkv_master - LEARNING_RATE * moment_new
    weight_bf16 = lax.all_gather(master_new.astype(jnp.bfloat16), "rep", axis=0, tiled=True)
    word_new = word_update(word_grads, token_ids, owner_map, word_master)
    return (error_new, right_basis, moment_new, master_new, weight_bf16, word_new)


def solution(mesh):
    in_specs = (
        P(("rep", "tp"), None),
        P("rep", "tp"),
        P("rep", None, "tp"),
        P("tp", None),
        P("rep", "tp"),
        P("rep", "tp"),
        P("rep", "tp"),
        P("rep"),
        P(),
        P("rep", "tp"),
    )
    out_specs = (
        P("rep", None, "tp"),
        P("tp", None),
        P("rep", "tp"),
        P("rep", "tp"),
        P(None, "tp"),
        P("rep", "tp"),
    )
    return jax.shard_map(shards, mesh=mesh, in_specs=in_specs, out_specs=out_specs, check_vma=False)
```

```python
import jax
import jax.numpy as jnp
from jax import lax
from jax.sharding import PartitionSpec as P

ROUNDS = 2


MOMENTUM = 0.9
LEARNING_RATE = 4.0
EMBED_RATE = 0.5


def tree_sum(value, axes):
    if isinstance(axes, str):
        axes = (axes,)
    count = 1
    for axis in axes:
        count *= lax.axis_size(axis)
    if count & (count - 1):
        return lax.psum(value, axes)
    stride = 1
    while stride < count:
        pairs = [(i, i ^ stride) for i in range(count)]
        value = value + lax.ppermute(value, axes, pairs)
        stride *= 2
    return value


def replica_product(block, out_grads, axis):
    count = lax.axis_size(axis)
    if count != 8 or block.shape[0] % 2:
        gathered = lax.all_gather(block, axis, axis=0, tiled=True)
        return lax.dot_general(
            gathered, out_grads, (((0,), (0,)), ((), ())), preferred_element_type=jnp.float32
        )
    me = lax.axis_index(axis)

    def exchange(value, stride):
        return lax.ppermute(value, axis, [(i, i ^ stride) for i in range(count)])

    from_x = exchange(block, 2)
    from_y = exchange(block, 4)
    diagonal = exchange(block, 6)
    mine = jnp.stack([block, from_x, from_y, diagonal])
    other = exchange(mine, 1)
    rows = block.shape[0]
    grads = out_grads.reshape(count, rows, out_grads.shape[1])
    even = jnp.stack([grads[me ^ offset] for offset in (0, 2, 4, 6)])
    odd = jnp.stack([grads[me ^ offset] for offset in (1, 3, 5, 7)])
    contract = (((0, 1), (0, 1)), ((), ()))
    first = lax.dot_general(mine, even, contract, preferred_element_type=jnp.float32)
    return first, (other, odd)


def split_tree_sum(value, axes):
    count = 1
    for axis in axes:
        count *= lax.axis_size(axis)
    rows = value.shape[0]
    if count & (count - 1) or count < 4 or rows % 2:
        return tree_sum(value, axes)

    def exchange(piece, stride):
        return lax.ppermute(piece, axes, [(i, i ^ stride) for i in range(count)])

    half = rows // 2
    core = lax.axis_index(axes[-1]) % 2
    kept = lax.dynamic_slice_in_dim(value, core * half, half, 0)
    given = lax.dynamic_slice_in_dim(value, (1 - core) * half, half, 0)
    kept = kept + exchange(given, 1)
    stride = 2
    while stride < count:
        kept = kept + exchange(kept, stride)
        stride *= 2
    other = exchange(kept, 1)
    total = jnp.zeros(value.shape, value.dtype)
    total = lax.dynamic_update_slice_in_dim(total, kept, core * half, 0)
    return lax.dynamic_update_slice_in_dim(total, other, (1 - core) * half, 0)


def orthonormal(left_basis, gram_matrix):
    factor_low = jnp.linalg.cholesky(gram_matrix)
    return jax.scipy.linalg.solve_triangular(factor_low, left_basis.T, lower=True).T


def word_update_dense(word_grads, token_ids, owner_map, word_master):
    replicas = lax.axis_size("rep")
    per_owner = word_master.shape[0]
    vocab = owner_map.shape[0]
    hits = token_ids[:, None] == jnp.arange(vocab, dtype=jnp.int32)[None, :]
    targets = jnp.sum(jnp.where(hits, owner_map[None, :], 0), axis=1)
    selector = (
        targets[:, None] == jnp.arange(replicas * per_owner, dtype=jnp.int32)[None, :]
    ).astype(jnp.bfloat16)
    partial = lax.dot_general(
        selector, word_grads, (((0,), (0,)), ((), ())), preferred_element_type=jnp.float32
    )
    me = lax.axis_index("rep")
    blocks = partial.reshape(replicas, per_owner, partial.shape[1])
    stride = 1
    while stride < replicas:
        bit = (me // stride) % 2
        paired = blocks.reshape((replicas // (2 * stride), 2) + blocks.shape[1:])
        kept = lax.dynamic_index_in_dim(paired, bit, axis=1, keepdims=False)
        sent = lax.dynamic_index_in_dim(paired, 1 - bit, axis=1, keepdims=False)
        pairs = [(i, i ^ stride) for i in range(replicas)]
        blocks = kept + lax.ppermute(sent, "rep", pairs)
        stride *= 2
    row_grad = blocks[0]
    return word_master - EMBED_RATE * row_grad


def word_update(word_grads, token_ids, owner_map, word_master):
    replicas = lax.axis_size("rep")
    if owner_map.shape[0] <= 4096 and replicas <= 8 and not replicas & (replicas - 1):
        return word_update_dense(word_grads, token_ids, owner_map, word_master)
    per_owner = word_master.shape[0]
    capacity = 2 * token_ids.shape[0] // replicas
    targets = owner_map[token_ids]
    owners = targets // per_owner
    row_slot = targets % per_owner
    matches = (owners[:, None] == jnp.arange(replicas, dtype=jnp.int32)[None, :]).astype(jnp.int32)
    places = jnp.sum(jnp.cumsum(matches, axis=0) * matches, axis=1) - 1
    outgoing = (
        jnp.zeros((replicas, capacity, word_grads.shape[1]), jnp.bfloat16)
        .at[owners, places]
        .set(word_grads)
    )
    labels = jnp.full((replicas, capacity), per_owner, jnp.int32).at[owners, places].set(row_slot)
    incoming, arrived = (
        lax.all_to_all(outgoing, "rep", split_axis=0, concat_axis=0, tiled=True),
        lax.all_to_all(labels, "rep", split_axis=0, concat_axis=0, tiled=True),
    )
    flat_rows = incoming.reshape(-1, incoming.shape[2])
    selector = (
        arrived.reshape(-1)[:, None] == jnp.arange(per_owner, dtype=jnp.int32)[None, :]
    ).astype(jnp.bfloat16)
    row_grad = lax.dot_general(
        selector, flat_rows, (((0,), (0,)), ((), ())), preferred_element_type=jnp.float32
    )
    return word_master - EMBED_RATE * row_grad


def shards(
    activations,
    out_grads,
    error_state,
    q_start,
    qkv_master,
    qkv_moment,
    word_grads,
    token_ids,
    owner_map,
    word_master,
):
    highest = lax.Precision.HIGHEST
    high = lax.Precision.HIGH
    replicas = lax.axis_size("rep")
    word_new = None
    early, late = replica_product(activations, out_grads, "tp")
    combined = early + error_state[0].astype(jnp.float32)
    right_rows = q_start.T
    left_rows = None
    for round_index in range(ROUNDS):
        partial_left = lax.dot_general(
            right_rows, combined, (((1,), (1,)), ((), ())), precision=high
        )
        if late is not None:
            other, odd = late
            partial_left, other = lax.optimization_barrier((partial_left, other))
            contract = (((0, 1), (0, 1)), ((), ()))
            second = lax.dot_general(other, odd, contract, preferred_element_type=jnp.float32)
            partial_left = partial_left + lax.dot_general(
                right_rows, second, (((1,), (1,)), ((), ())), precision=high
            )
            combined = combined + second
            late = None
        left_rows = split_tree_sum(partial_left, ("rep", "tp")) / replicas
        gram_matrix = jnp.dot(left_rows, left_rows.T, precision=highest)
        factor_low = jnp.linalg.cholesky(gram_matrix)
        left_rows = jax.scipy.linalg.solve_triangular(factor_low, left_rows, lower=True)
        partial_right = jnp.dot(left_rows, combined, precision=high)
        right_rows = tree_sum(partial_right, "rep") / replicas
    right_basis = right_rows.T
    approx = lax.dot_general(
        left_rows, right_rows, (((0,), (0,)), ((), ())), precision=high
    )
    error_new = (combined - approx).astype(jnp.bfloat16)[None]
    owned_rows = qkv_master.shape[0]
    update_rows = lax.dynamic_slice_in_dim(
        approx, lax.axis_index("rep") * owned_rows, owned_rows, 0
    )
    moment_new = MOMENTUM * qkv_moment + update_rows
    master_new = qkv_master - LEARNING_RATE * moment_new
    weight_bf16 = lax.all_gather(master_new.astype(jnp.bfloat16), "rep", axis=0, tiled=True)
    word_new = word_update(word_grads, token_ids, owner_map, word_master)
    return (error_new, right_basis, moment_new, master_new, weight_bf16, word_new)


def solution(mesh):
    in_specs = (
        P(("rep", "tp"), None),
        P("rep", "tp"),
        P("rep", None, "tp"),
        P("tp", None),
        P("rep", "tp"),
        P("rep", "tp"),
        P("rep", "tp"),
        P("rep"),
        P(),
        P("rep", "tp"),
    )
    out_specs = (
        P("rep", None, "tp"),
        P("tp", None),
        P("rep", "tp"),
        P("rep", "tp"),
        P(None, "tp"),
        P("rep", "tp"),
    )
    return jax.shard_map(shards, mesh=mesh, in_specs=in_specs, out_specs=out_specs, check_vma=False)
```

```python
import jax
import jax.numpy as jnp
from jax import lax
from jax.sharding import PartitionSpec as P

ROUNDS = 2


MOMENTUM = 0.9
LEARNING_RATE = 4.0
EMBED_RATE = 0.5


def tree_sum(value, axes):
    if isinstance(axes, str):
        axes = (axes,)
    count = 1
    for axis in axes:
        count *= lax.axis_size(axis)
    if count & (count - 1):
        return lax.psum(value, axes)
    stride = 1
    while stride < count:
        pairs = [(i, i ^ stride) for i in range(count)]
        value = value + lax.ppermute(value, axes, pairs)
        stride *= 2
    return value


def replica_product(block, out_grads, axis):
    count = lax.axis_size(axis)
    if count != 8 or block.shape[0] % 2:
        gathered = lax.all_gather(block, axis, axis=0, tiled=True)
        return lax.dot_general(
            gathered, out_grads, (((0,), (0,)), ((), ())), preferred_element_type=jnp.float32
        )
    me = lax.axis_index(axis)

    def exchange(value, stride):
        return lax.ppermute(value, axis, [(i, i ^ stride) for i in range(count)])

    from_x = exchange(block, 2)
    from_y = exchange(block, 4)
    half = block.shape[0] // 2
    diagonal = jnp.concatenate(
        [exchange(from_y[:half], 2), exchange(from_x[half:], 4)], axis=0
    )
    mine = jnp.stack([block, from_x, from_y, diagonal])
    other = exchange(mine, 1)
    rows = block.shape[0]
    grads = out_grads.reshape(count, rows, out_grads.shape[1])
    even = jnp.stack([grads[me ^ offset] for offset in (0, 2, 4, 6)])
    odd = jnp.stack([grads[me ^ offset] for offset in (1, 3, 5, 7)])
    contract = (((0, 1), (0, 1)), ((), ()))
    first = lax.dot_general(mine, even, contract, preferred_element_type=jnp.float32)
    return first, (other, odd)


def split_tree_sum(value, axes):
    count = 1
    for axis in axes:
        count *= lax.axis_size(axis)
    rows = value.shape[0]
    if count & (count - 1) or count < 4 or rows % 2:
        return tree_sum(value, axes)

    def exchange(piece, stride):
        return lax.ppermute(piece, axes, [(i, i ^ stride) for i in range(count)])

    half = rows // 2
    core = lax.axis_index(axes[-1]) % 2
    kept = lax.dynamic_slice_in_dim(value, core * half, half, 0)
    given = lax.dynamic_slice_in_dim(value, (1 - core) * half, half, 0)
    kept = kept + exchange(given, 1)
    stride = 2
    while stride < count:
        kept = kept + exchange(kept, stride)
        stride *= 2
    other = exchange(kept, 1)
    total = jnp.zeros(value.shape, value.dtype)
    total = lax.dynamic_update_slice_in_dim(total, kept, core * half, 0)
    return lax.dynamic_update_slice_in_dim(total, other, (1 - core) * half, 0)


def orthonormal(left_basis, gram_matrix):
    factor_low = jnp.linalg.cholesky(gram_matrix)
    return jax.scipy.linalg.solve_triangular(factor_low, left_basis.T, lower=True).T


def word_update_dense(word_grads, token_ids, owner_map, word_master):
    replicas = lax.axis_size("rep")
    per_owner = word_master.shape[0]
    vocab = owner_map.shape[0]
    hits = token_ids[:, None] == jnp.arange(vocab, dtype=jnp.int32)[None, :]
    targets = jnp.sum(jnp.where(hits, owner_map[None, :], 0), axis=1)
    selector = (
        targets[:, None] == jnp.arange(replicas * per_owner, dtype=jnp.int32)[None, :]
    ).astype(jnp.bfloat16)
    partial = lax.dot_general(
        selector, word_grads, (((0,), (0,)), ((), ())), preferred_element_type=jnp.float32
    )
    me = lax.axis_index("rep")
    blocks = partial.reshape(replicas, per_owner, partial.shape[1])
    stride = 1
    while stride < replicas:
        bit = (me // stride) % 2
        paired = blocks.reshape((replicas // (2 * stride), 2) + blocks.shape[1:])
        kept = lax.dynamic_index_in_dim(paired, bit, axis=1, keepdims=False)
        sent = lax.dynamic_index_in_dim(paired, 1 - bit, axis=1, keepdims=False)
        pairs = [(i, i ^ stride) for i in range(replicas)]
        blocks = kept + lax.ppermute(sent, "rep", pairs)
        stride *= 2
    row_grad = blocks[0]
    return word_master - EMBED_RATE * row_grad


def word_update(word_grads, token_ids, owner_map, word_master):
    replicas = lax.axis_size("rep")
    if owner_map.shape[0] <= 4096 and replicas <= 8 and not replicas & (replicas - 1):
        return word_update_dense(word_grads, token_ids, owner_map, word_master)
    per_owner = word_master.shape[0]
    capacity = 2 * token_ids.shape[0] // replicas
    targets = owner_map[token_ids]
    owners = targets // per_owner
    row_slot = targets % per_owner
    matches = (owners[:, None] == jnp.arange(replicas, dtype=jnp.int32)[None, :]).astype(jnp.int32)
    places = jnp.sum(jnp.cumsum(matches, axis=0) * matches, axis=1) - 1
    outgoing = (
        jnp.zeros((replicas, capacity, word_grads.shape[1]), jnp.bfloat16)
        .at[owners, places]
        .set(word_grads)
    )
    labels = jnp.full((replicas, capacity), per_owner, jnp.int32).at[owners, places].set(row_slot)
    incoming, arrived = (
        lax.all_to_all(outgoing, "rep", split_axis=0, concat_axis=0, tiled=True),
        lax.all_to_all(labels, "rep", split_axis=0, concat_axis=0, tiled=True),
    )
    flat_rows = incoming.reshape(-1, incoming.shape[2])
    selector = (
        arrived.reshape(-1)[:, None] == jnp.arange(per_owner, dtype=jnp.int32)[None, :]
    ).astype(jnp.bfloat16)
    row_grad = lax.dot_general(
        selector, flat_rows, (((0,), (0,)), ((), ())), preferred_element_type=jnp.float32
    )
    return word_master - EMBED_RATE * row_grad


def shards(
    activations,
    out_grads,
    error_state,
    q_start,
    qkv_master,
    qkv_moment,
    word_grads,
    token_ids,
    owner_map,
    word_master,
):
    highest = lax.Precision.HIGHEST
    high = lax.Precision.HIGH
    replicas = lax.axis_size("rep")
    word_new = None
    early, late = replica_product(activations, out_grads, "tp")
    combined = early + error_state[0].astype(jnp.float32)
    right_rows = q_start.T
    left_rows = None
    for round_index in range(ROUNDS):
        partial_left = lax.dot_general(
            right_rows, combined, (((1,), (1,)), ((), ())), precision=high
        )
        if late is not None:
            other, odd = late
            partial_left, other = lax.optimization_barrier((partial_left, other))
            contract = (((0, 1), (0, 1)), ((), ()))
            second = lax.dot_general(other, odd, contract, preferred_element_type=jnp.float32)
            partial_left = partial_left + lax.dot_general(
                right_rows, second, (((1,), (1,)), ((), ())), precision=high
            )
            combined = combined + second
            late = None
        left_rows = split_tree_sum(partial_left, ("rep", "tp")) / replicas
        gram_matrix = jnp.dot(left_rows, left_rows.T, precision=highest)
        factor_low = jnp.linalg.cholesky(gram_matrix)
        inverse_low = jax.scipy.linalg.solve_triangular(
            factor_low, jnp.eye(factor_low.shape[0], dtype=factor_low.dtype), lower=True
        )
        left_rows = jnp.dot(inverse_low, left_rows, precision=highest)
        partial_right = jnp.dot(left_rows, combined, precision=high)
        right_rows = tree_sum(partial_right, "rep") / replicas
    right_basis = right_rows.T
    approx = lax.dot_general(
        left_rows, right_rows, (((0,), (0,)), ((), ())), precision=high
    )
    error_new = (combined - approx).astype(jnp.bfloat16)[None]
    owned_rows = qkv_master.shape[0]
    update_rows = lax.dynamic_slice_in_dim(
        approx, lax.axis_index("rep") * owned_rows, owned_rows, 0
    )
    moment_new = MOMENTUM * qkv_moment + update_rows
    master_new = qkv_master - LEARNING_RATE * moment_new
    weight_bf16 = lax.all_gather(master_new.astype(jnp.bfloat16), "rep", axis=0, tiled=True)
    word_new = word_update(word_grads, token_ids, owner_map, word_master)
    return (error_new, right_basis, moment_new, master_new, weight_bf16, word_new)


def solution(mesh):
    in_specs = (
        P(("rep", "tp"), None),
        P("rep", "tp"),
        P("rep", None, "tp"),
        P("tp", None),
        P("rep", "tp"),
        P("rep", "tp"),
        P("rep", "tp"),
        P("rep"),
        P(),
        P("rep", "tp"),
    )
    out_specs = (
        P("rep", None, "tp"),
        P("tp", None),
        P("rep", "tp"),
        P("rep", "tp"),
        P(None, "tp"),
        P("rep", "tp"),
    )
    return jax.shard_map(shards, mesh=mesh, in_specs=in_specs, out_specs=out_specs, check_vma=False)
```

```python
import jax
import jax.numpy as jnp
from jax import lax
from jax.sharding import PartitionSpec as P

ROUNDS = 2


MOMENTUM = 0.9
LEARNING_RATE = 4.0
EMBED_RATE = 0.5


def tree_sum(value, axes):
    if isinstance(axes, str):
        axes = (axes,)
    count = 1
    for axis in axes:
        count *= lax.axis_size(axis)
    if count & (count - 1):
        return lax.psum(value, axes)
    stride = 1
    while stride < count:
        pairs = [(i, i ^ stride) for i in range(count)]
        value = value + lax.ppermute(value, axes, pairs)
        stride *= 2
    return value


def replica_product(block, out_grads, axis):
    count = lax.axis_size(axis)
    if count != 8 or block.shape[0] % 2:
        gathered = lax.all_gather(block, axis, axis=0, tiled=True)
        return lax.dot_general(
            gathered, out_grads, (((0,), (0,)), ((), ())), preferred_element_type=jnp.float32
        )
    me = lax.axis_index(axis)

    def exchange(value, stride):
        return lax.ppermute(value, axis, [(i, i ^ stride) for i in range(count)])

    from_x = exchange(block, 2)
    from_y = exchange(block, 4)
    half = block.shape[0] // 2
    diagonal = jnp.concatenate(
        [exchange(from_y[:half], 2), exchange(from_x[half:], 4)], axis=0
    )
    mine = jnp.stack([block, from_x, from_y, diagonal])
    other = exchange(mine, 1)
    rows = block.shape[0]
    grads = out_grads.reshape(count, rows, out_grads.shape[1])
    even = jnp.stack([grads[me ^ offset] for offset in (0, 2, 4, 6)])
    odd = jnp.stack([grads[me ^ offset] for offset in (1, 3, 5, 7)])
    contract = (((0, 1), (0, 1)), ((), ()))
    first = lax.dot_general(mine, even, contract, preferred_element_type=jnp.float32)
    return first, (other, odd)


def split_tree_sum(value, axes):
    count = 1
    for axis in axes:
        count *= lax.axis_size(axis)
    rows = value.shape[0]
    if count & (count - 1) or count < 4 or rows % 2:
        return tree_sum(value, axes)

    def exchange(piece, stride):
        return lax.ppermute(piece, axes, [(i, i ^ stride) for i in range(count)])

    half = rows // 2
    core = lax.axis_index(axes[-1]) % 2
    kept = lax.dynamic_slice_in_dim(value, core * half, half, 0)
    given = lax.dynamic_slice_in_dim(value, (1 - core) * half, half, 0)
    kept = kept + exchange(given, 1)
    stride = 2
    if count >= 8:
        kept = (kept + exchange(kept, 2)) + (exchange(kept, 4) + exchange(kept, 6))
        stride = 8
    while stride < count:
        kept = kept + exchange(kept, stride)
        stride *= 2
    other = exchange(kept, 1)
    total = jnp.zeros(value.shape, value.dtype)
    total = lax.dynamic_update_slice_in_dim(total, kept, core * half, 0)
    return lax.dynamic_update_slice_in_dim(total, other, (1 - core) * half, 0)


def orthonormal(left_basis, gram_matrix):
    factor_low = jnp.linalg.cholesky(gram_matrix)
    return jax.scipy.linalg.solve_triangular(factor_low, left_basis.T, lower=True).T


def word_update_dense(word_grads, token_ids, owner_map, word_master):
    replicas = lax.axis_size("rep")
    per_owner = word_master.shape[0]
    vocab = owner_map.shape[0]
    hits = token_ids[:, None] == jnp.arange(vocab, dtype=jnp.int32)[None, :]
    targets = jnp.sum(jnp.where(hits, owner_map[None, :], 0), axis=1)
    selector = (
        targets[:, None] == jnp.arange(replicas * per_owner, dtype=jnp.int32)[None, :]
    ).astype(jnp.bfloat16)
    partial = lax.dot_general(
        selector, word_grads, (((0,), (0,)), ((), ())), preferred_element_type=jnp.float32
    )
    me = lax.axis_index("rep")
    blocks = partial.reshape(replicas, per_owner, partial.shape[1])
    stride = 1
    while stride < replicas:
        bit = (me // stride) % 2
        paired = blocks.reshape((replicas // (2 * stride), 2) + blocks.shape[1:])
        kept = lax.dynamic_index_in_dim(paired, bit, axis=1, keepdims=False)
        sent = lax.dynamic_index_in_dim(paired, 1 - bit, axis=1, keepdims=False)
        pairs = [(i, i ^ stride) for i in range(replicas)]
        blocks = kept + lax.ppermute(sent, "rep", pairs)
        stride *= 2
    row_grad = blocks[0]
    return word_master - EMBED_RATE * row_grad


def word_update(word_grads, token_ids, owner_map, word_master):
    replicas = lax.axis_size("rep")
    if owner_map.shape[0] <= 4096 and replicas <= 8 and not replicas & (replicas - 1):
        return word_update_dense(word_grads, token_ids, owner_map, word_master)
    per_owner = word_master.shape[0]
    capacity = 2 * token_ids.shape[0] // replicas
    targets = owner_map[token_ids]
    owners = targets // per_owner
    row_slot = targets % per_owner
    matches = (owners[:, None] == jnp.arange(replicas, dtype=jnp.int32)[None, :]).astype(jnp.int32)
    places = jnp.sum(jnp.cumsum(matches, axis=0) * matches, axis=1) - 1
    outgoing = (
        jnp.zeros((replicas, capacity, word_grads.shape[1]), jnp.bfloat16)
        .at[owners, places]
        .set(word_grads)
    )
    labels = jnp.full((replicas, capacity), per_owner, jnp.int32).at[owners, places].set(row_slot)
    incoming, arrived = (
        lax.all_to_all(outgoing, "rep", split_axis=0, concat_axis=0, tiled=True),
        lax.all_to_all(labels, "rep", split_axis=0, concat_axis=0, tiled=True),
    )
    flat_rows = incoming.reshape(-1, incoming.shape[2])
    selector = (
        arrived.reshape(-1)[:, None] == jnp.arange(per_owner, dtype=jnp.int32)[None, :]
    ).astype(jnp.bfloat16)
    row_grad = lax.dot_general(
        selector, flat_rows, (((0,), (0,)), ((), ())), preferred_element_type=jnp.float32
    )
    return word_master - EMBED_RATE * row_grad


def shards(
    activations,
    out_grads,
    error_state,
    q_start,
    qkv_master,
    qkv_moment,
    word_grads,
    token_ids,
    owner_map,
    word_master,
):
    highest = lax.Precision.HIGHEST
    high = lax.Precision.HIGH
    replicas = lax.axis_size("rep")
    word_new = None
    early, late = replica_product(activations, out_grads, "tp")
    combined = early + error_state[0].astype(jnp.float32)
    right_rows = q_start.T
    left_rows = None
    for round_index in range(ROUNDS):
        partial_left = lax.dot_general(
            right_rows, combined, (((1,), (1,)), ((), ())), precision=high
        )
        if late is not None:
            other, odd = late
            partial_left, other = lax.optimization_barrier((partial_left, other))
            contract = (((0, 1), (0, 1)), ((), ()))
            second = lax.dot_general(other, odd, contract, preferred_element_type=jnp.float32)
            partial_left = partial_left + lax.dot_general(
                right_rows, second, (((1,), (1,)), ((), ())), precision=high
            )
            combined = combined + second
            late = None
        left_rows = split_tree_sum(partial_left, ("rep", "tp")) / replicas
        gram_matrix = jnp.dot(left_rows, left_rows.T, precision=highest)
        factor_low = jnp.linalg.cholesky(gram_matrix)
        left_rows = jax.scipy.linalg.solve_triangular(factor_low, left_rows, lower=True)
        partial_right = jnp.dot(left_rows, combined, precision=high)
        right_rows = tree_sum(partial_right, "rep") / replicas
    right_basis = right_rows.T
    approx = lax.dot_general(
        left_rows, right_rows, (((0,), (0,)), ((), ())), precision=high
    )
    error_new = (combined - approx).astype(jnp.bfloat16)[None]
    owned_rows = qkv_master.shape[0]
    update_rows = lax.dynamic_slice_in_dim(
        approx, lax.axis_index("rep") * owned_rows, owned_rows, 0
    )
    moment_new = MOMENTUM * qkv_moment + update_rows
    master_new = qkv_master - LEARNING_RATE * moment_new
    weight_bf16 = lax.all_gather(master_new.astype(jnp.bfloat16), "rep", axis=0, tiled=True)
    word_new = word_update(word_grads, token_ids, owner_map, word_master)
    return (error_new, right_basis, moment_new, master_new, weight_bf16, word_new)


def solution(mesh):
    in_specs = (
        P(("rep", "tp"), None),
        P("rep", "tp"),
        P("rep", None, "tp"),
        P("tp", None),
        P("rep", "tp"),
        P("rep", "tp"),
        P("rep", "tp"),
        P("rep"),
        P(),
        P("rep", "tp"),
    )
    out_specs = (
        P("rep", None, "tp"),
        P("tp", None),
        P("rep", "tp"),
        P("rep", "tp"),
        P(None, "tp"),
        P("rep", "tp"),
    )
    return jax.shard_map(shards, mesh=mesh, in_specs=in_specs, out_specs=out_specs, check_vma=False)
```

```python
import jax
import jax.numpy as jnp
from jax import lax
from jax.sharding import PartitionSpec as P

ROUNDS = 2


MOMENTUM = 0.9
LEARNING_RATE = 4.0
EMBED_RATE = 0.5


def tree_sum(value, axes):
    if isinstance(axes, str):
        axes = (axes,)
    count = 1
    for axis in axes:
        count *= lax.axis_size(axis)
    if count & (count - 1):
        return lax.psum(value, axes)
    stride = 1
    while stride < count:
        pairs = [(i, i ^ stride) for i in range(count)]
        value = value + lax.ppermute(value, axes, pairs)
        stride *= 2
    return value


def replica_product(block, out_grads, axis):
    count = lax.axis_size(axis)
    if count != 8 or block.shape[0] % 2:
        gathered = lax.all_gather(block, axis, axis=0, tiled=True)
        return lax.dot_general(
            gathered, out_grads, (((0,), (0,)), ((), ())), preferred_element_type=jnp.float32
        )
    me = lax.axis_index(axis)

    def exchange(value, stride):
        return lax.ppermute(value, axis, [(i, i ^ stride) for i in range(count)])

    from_x = exchange(block, 2)
    from_y = exchange(block, 4)
    half = block.shape[0] // 2
    diagonal = jnp.concatenate(
        [exchange(from_y[:half], 2), exchange(from_x[half:], 4)], axis=0
    )
    mine = jnp.stack([block, from_x, from_y, diagonal])
    other = exchange(mine, 1)
    rows = block.shape[0]
    grads = out_grads.reshape(count, rows, out_grads.shape[1])
    even = jnp.stack([grads[me ^ offset] for offset in (0, 2, 4, 6)])
    odd = jnp.stack([grads[me ^ offset] for offset in (1, 3, 5, 7)])
    contract = (((0, 1), (0, 1)), ((), ()))
    first = lax.dot_general(mine, even, contract, preferred_element_type=jnp.float32)
    return first, (other, odd)


def split_tree_sum(value, axes):
    count = 1
    for axis in axes:
        count *= lax.axis_size(axis)
    rows = value.shape[0]
    if count & (count - 1) or count < 4 or rows % 2:
        return tree_sum(value, axes)

    def exchange(piece, stride):
        return lax.ppermute(piece, axes, [(i, i ^ stride) for i in range(count)])

    half = rows // 2
    core = lax.axis_index(axes[-1]) % 2
    kept = lax.dynamic_slice_in_dim(value, core * half, half, 0)
    given = lax.dynamic_slice_in_dim(value, (1 - core) * half, half, 0)
    kept = kept + exchange(given, 1)
    stride = 2
    if count >= 8:
        kept = (kept + exchange(kept, 2)) + (exchange(kept, 4) + exchange(kept, 6))
        stride = 8
    while stride < count:
        kept = kept + exchange(kept, stride)
        stride *= 2
    other = exchange(kept, 1)
    total = jnp.zeros(value.shape, value.dtype)
    total = lax.dynamic_update_slice_in_dim(total, kept, core * half, 0)
    return lax.dynamic_update_slice_in_dim(total, other, (1 - core) * half, 0)


def orthonormal(left_basis, gram_matrix):
    factor_low = jnp.linalg.cholesky(gram_matrix)
    return jax.scipy.linalg.solve_triangular(factor_low, left_basis.T, lower=True).T


def word_update_dense(word_grads, token_ids, owner_map, word_master):
    replicas = lax.axis_size("rep")
    per_owner = word_master.shape[0]
    vocab = owner_map.shape[0]
    hits = token_ids[:, None] == jnp.arange(vocab, dtype=jnp.int32)[None, :]
    targets = jnp.sum(jnp.where(hits, owner_map[None, :], 0), axis=1)
    selector = (
        targets[:, None] == jnp.arange(replicas * per_owner, dtype=jnp.int32)[None, :]
    ).astype(jnp.bfloat16)
    partial = lax.dot_general(
        selector, word_grads, (((0,), (0,)), ((), ())), preferred_element_type=jnp.float32
    )
    me = lax.axis_index("rep")
    blocks = partial.reshape(replicas, per_owner, partial.shape[1])
    stride = 1
    while stride < replicas:
        bit = (me // stride) % 2
        paired = blocks.reshape((replicas // (2 * stride), 2) + blocks.shape[1:])
        kept = lax.dynamic_index_in_dim(paired, bit, axis=1, keepdims=False)
        sent = lax.dynamic_index_in_dim(paired, 1 - bit, axis=1, keepdims=False)
        pairs = [(i, i ^ stride) for i in range(replicas)]
        blocks = kept + lax.ppermute(sent, "rep", pairs)
        stride *= 2
    row_grad = blocks[0]
    return word_master - EMBED_RATE * row_grad


def word_update(word_grads, token_ids, owner_map, word_master):
    replicas = lax.axis_size("rep")
    if owner_map.shape[0] <= 4096 and replicas <= 8 and not replicas & (replicas - 1):
        return word_update_dense(word_grads, token_ids, owner_map, word_master)
    per_owner = word_master.shape[0]
    capacity = 2 * token_ids.shape[0] // replicas
    targets = owner_map[token_ids]
    owners = targets // per_owner
    row_slot = targets % per_owner
    matches = (owners[:, None] == jnp.arange(replicas, dtype=jnp.int32)[None, :]).astype(jnp.int32)
    places = jnp.sum(jnp.cumsum(matches, axis=0) * matches, axis=1) - 1
    outgoing = (
        jnp.zeros((replicas, capacity, word_grads.shape[1]), jnp.bfloat16)
        .at[owners, places]
        .set(word_grads)
    )
    labels = jnp.full((replicas, capacity), per_owner, jnp.int32).at[owners, places].set(row_slot)
    incoming, arrived = (
        lax.all_to_all(outgoing, "rep", split_axis=0, concat_axis=0, tiled=True),
        lax.all_to_all(labels, "rep", split_axis=0, concat_axis=0, tiled=True),
    )
    flat_rows = incoming.reshape(-1, incoming.shape[2])
    selector = (
        arrived.reshape(-1)[:, None] == jnp.arange(per_owner, dtype=jnp.int32)[None, :]
    ).astype(jnp.bfloat16)
    row_grad = lax.dot_general(
        selector, flat_rows, (((0,), (0,)), ((), ())), preferred_element_type=jnp.float32
    )
    return word_master - EMBED_RATE * row_grad


def shards(
    activations,
    out_grads,
    error_state,
    q_start,
    qkv_master,
    qkv_moment,
    word_grads,
    token_ids,
    owner_map,
    word_master,
):
    highest = lax.Precision.HIGHEST
    high = lax.Precision.HIGH
    replicas = lax.axis_size("rep")
    word_new = None
    early, late = replica_product(activations, out_grads, "tp")
    combined = early + error_state[0].astype(jnp.float32)
    right_rows = q_start.T
    left_rows = None
    for round_index in range(ROUNDS):
        partial_left = lax.dot_general(
            right_rows, combined, (((1,), (1,)), ((), ())), precision=high
        )
        if late is not None:
            other, odd = late
            partial_left, other = lax.optimization_barrier((partial_left, other))
            contract = (((0, 1), (0, 1)), ((), ()))
            second = lax.dot_general(other, odd, contract, preferred_element_type=jnp.float32)
            partial_left = partial_left + lax.dot_general(
                right_rows, second, (((1,), (1,)), ((), ())), precision=high
            )
            combined = combined + second
            late = None
        left_rows = split_tree_sum(partial_left, ("rep", "tp")) / replicas
        gram_matrix = jnp.dot(left_rows, left_rows.T, precision=high)
        factor_low = lax.linalg.cholesky(gram_matrix, symmetrize_input=False)
        left_rows = jax.scipy.linalg.solve_triangular(factor_low, left_rows, lower=True)
        partial_right = jnp.dot(left_rows, combined, precision=high)
        right_rows = tree_sum(partial_right, "rep") / replicas
    right_basis = right_rows.T
    approx = lax.dot_general(
        left_rows, right_rows, (((0,), (0,)), ((), ())), precision=high
    )
    error_new = (combined - approx).astype(jnp.bfloat16)[None]
    owned_rows = qkv_master.shape[0]
    update_rows = lax.dynamic_slice_in_dim(
        approx, lax.axis_index("rep") * owned_rows, owned_rows, 0
    )
    moment_new = MOMENTUM * qkv_moment + update_rows
    master_new = qkv_master - LEARNING_RATE * moment_new
    weight_bf16 = lax.all_gather(master_new.astype(jnp.bfloat16), "rep", axis=0, tiled=True)
    word_new = word_update(word_grads, token_ids, owner_map, word_master)
    return (error_new, right_basis, moment_new, master_new, weight_bf16, word_new)


def solution(mesh):
    in_specs = (
        P(("rep", "tp"), None),
        P("rep", "tp"),
        P("rep", None, "tp"),
        P("tp", None),
        P("rep", "tp"),
        P("rep", "tp"),
        P("rep", "tp"),
        P("rep"),
        P(),
        P("rep", "tp"),
    )
    out_specs = (
        P("rep", None, "tp"),
        P("tp", None),
        P("rep", "tp"),
        P("rep", "tp"),
        P(None, "tp"),
        P("rep", "tp"),
    )
    return jax.shard_map(shards, mesh=mesh, in_specs=in_specs, out_specs=out_specs, check_vma=False)
```

```python
import jax
import jax.numpy as jnp
from jax import lax
from jax.sharding import PartitionSpec as P

ROUNDS = 2


MOMENTUM = 0.9
LEARNING_RATE = 4.0
EMBED_RATE = 0.5


def tree_sum(value, axes):
    if isinstance(axes, str):
        axes = (axes,)
    count = 1
    for axis in axes:
        count *= lax.axis_size(axis)
    if count & (count - 1):
        return lax.psum(value, axes)
    stride = 1
    while stride < count:
        pairs = [(i, i ^ stride) for i in range(count)]
        value = value + lax.ppermute(value, axes, pairs)
        stride *= 2
    return value


def replica_product(block, out_grads, axis):
    count = lax.axis_size(axis)
    if count != 8 or block.shape[0] % 2:
        gathered = lax.all_gather(block, axis, axis=0, tiled=True)
        return lax.dot_general(
            gathered, out_grads, (((0,), (0,)), ((), ())), preferred_element_type=jnp.float32
        )
    me = lax.axis_index(axis)

    def exchange(value, stride):
        return lax.ppermute(value, axis, [(i, i ^ stride) for i in range(count)])

    from_x = exchange(block, 2)
    from_y = exchange(block, 4)
    half = block.shape[0] // 2
    diagonal = jnp.concatenate(
        [exchange(from_y[:half], 2), exchange(from_x[half:], 4)], axis=0
    )
    mine = jnp.stack([block, from_x, from_y, diagonal])
    other = exchange(mine, 1)
    rows = block.shape[0]
    grads = out_grads.reshape(count, rows, out_grads.shape[1])
    even = jnp.stack([grads[me ^ offset] for offset in (0, 2, 4, 6)])
    odd = jnp.stack([grads[me ^ offset] for offset in (1, 3, 5, 7)])
    contract = (((0, 1), (0, 1)), ((), ()))
    first = lax.dot_general(mine, even, contract, preferred_element_type=jnp.float32)
    return first, (other, odd)


def split_tree_sum(value, axes):
    count = 1
    for axis in axes:
        count *= lax.axis_size(axis)
    rows = value.shape[0]
    if count & (count - 1) or count < 4 or rows % 2:
        return tree_sum(value, axes)

    def exchange(piece, stride):
        return lax.ppermute(piece, axes, [(i, i ^ stride) for i in range(count)])

    half = rows // 2
    core = lax.axis_index(axes[-1]) % 2
    kept = lax.dynamic_slice_in_dim(value, core * half, half, 0)
    given = lax.dynamic_slice_in_dim(value, (1 - core) * half, half, 0)
    kept = kept + exchange(given, 1)
    stride = 2
    while 4 * stride <= count:
        low, high = stride, 2 * stride
        kept = (kept + exchange(kept, low)) + (exchange(kept, high) + exchange(kept, low ^ high))
        stride *= 4
    while stride < count:
        kept = kept + exchange(kept, stride)
        stride *= 2
    other = exchange(kept, 1)
    total = jnp.zeros(value.shape, value.dtype)
    total = lax.dynamic_update_slice_in_dim(total, kept, core * half, 0)
    return lax.dynamic_update_slice_in_dim(total, other, (1 - core) * half, 0)


def orthonormal(left_basis, gram_matrix):
    factor_low = jnp.linalg.cholesky(gram_matrix)
    return jax.scipy.linalg.solve_triangular(factor_low, left_basis.T, lower=True).T


def word_update_dense(word_grads, token_ids, owner_map, word_master):
    replicas = lax.axis_size("rep")
    per_owner = word_master.shape[0]
    vocab = owner_map.shape[0]
    hits = token_ids[:, None] == jnp.arange(vocab, dtype=jnp.int32)[None, :]
    targets = jnp.sum(jnp.where(hits, owner_map[None, :], 0), axis=1)
    selector = (
        targets[:, None] == jnp.arange(replicas * per_owner, dtype=jnp.int32)[None, :]
    ).astype(jnp.bfloat16)
    partial = lax.dot_general(
        selector, word_grads, (((0,), (0,)), ((), ())), preferred_element_type=jnp.float32
    )
    me = lax.axis_index("rep")
    blocks = partial.reshape(replicas, per_owner, partial.shape[1])
    stride = 1
    while stride < replicas:
        bit = (me // stride) % 2
        paired = blocks.reshape((replicas // (2 * stride), 2) + blocks.shape[1:])
        kept = lax.dynamic_index_in_dim(paired, bit, axis=1, keepdims=False)
        sent = lax.dynamic_index_in_dim(paired, 1 - bit, axis=1, keepdims=False)
        pairs = [(i, i ^ stride) for i in range(replicas)]
        blocks = kept + lax.ppermute(sent, "rep", pairs)
        stride *= 2
    row_grad = blocks[0]
    return word_master - EMBED_RATE * row_grad


def word_update(word_grads, token_ids, owner_map, word_master):
    replicas = lax.axis_size("rep")
    if owner_map.shape[0] <= 4096 and replicas <= 8 and not replicas & (replicas - 1):
        return word_update_dense(word_grads, token_ids, owner_map, word_master)
    per_owner = word_master.shape[0]
    capacity = 2 * token_ids.shape[0] // replicas
    targets = owner_map[token_ids]
    owners = targets // per_owner
    row_slot = targets % per_owner
    matches = (owners[:, None] == jnp.arange(replicas, dtype=jnp.int32)[None, :]).astype(jnp.int32)
    places = jnp.sum(jnp.cumsum(matches, axis=0) * matches, axis=1) - 1
    outgoing = (
        jnp.zeros((replicas, capacity, word_grads.shape[1]), jnp.bfloat16)
        .at[owners, places]
        .set(word_grads)
    )
    labels = jnp.full((replicas, capacity), per_owner, jnp.int32).at[owners, places].set(row_slot)
    incoming, arrived = (
        lax.all_to_all(outgoing, "rep", split_axis=0, concat_axis=0, tiled=True),
        lax.all_to_all(labels, "rep", split_axis=0, concat_axis=0, tiled=True),
    )
    flat_rows = incoming.reshape(-1, incoming.shape[2])
    selector = (
        arrived.reshape(-1)[:, None] == jnp.arange(per_owner, dtype=jnp.int32)[None, :]
    ).astype(jnp.bfloat16)
    row_grad = lax.dot_general(
        selector, flat_rows, (((0,), (0,)), ((), ())), preferred_element_type=jnp.float32
    )
    return word_master - EMBED_RATE * row_grad


def shards(
    activations,
    out_grads,
    error_state,
    q_start,
    qkv_master,
    qkv_moment,
    word_grads,
    token_ids,
    owner_map,
    word_master,
):
    highest = lax.Precision.HIGHEST
    high = lax.Precision.HIGH
    replicas = lax.axis_size("rep")
    word_new = None
    early, late = replica_product(activations, out_grads, "tp")
    combined = early + error_state[0].astype(jnp.float32)
    right_rows = q_start.T
    left_rows = None
    for round_index in range(ROUNDS):
        partial_left = lax.dot_general(
            right_rows, combined, (((1,), (1,)), ((), ())), precision=high
        )
        if late is not None:
            other, odd = late
            partial_left, other = lax.optimization_barrier((partial_left, other))
            contract = (((0, 1), (0, 1)), ((), ()))
            second = lax.dot_general(other, odd, contract, preferred_element_type=jnp.float32)
            partial_left = partial_left + lax.dot_general(
                right_rows, second, (((1,), (1,)), ((), ())), precision=high
            )
            combined = combined + second
            late = None
        left_rows = split_tree_sum(partial_left, ("rep", "tp")) / replicas
        gram_matrix = jnp.dot(left_rows, left_rows.T, precision=high)
        factor_low = lax.linalg.cholesky(gram_matrix, symmetrize_input=False)
        left_rows = jax.scipy.linalg.solve_triangular(factor_low, left_rows, lower=True)
        partial_right = jnp.dot(left_rows, combined, precision=high)
        right_rows = tree_sum(partial_right, "rep") / replicas
    right_basis = right_rows.T
    approx = lax.dot_general(
        left_rows, right_rows, (((0,), (0,)), ((), ())), precision=high
    )
    error_new = (combined - approx).astype(jnp.bfloat16)[None]
    owned_rows = qkv_master.shape[0]
    update_rows = lax.dynamic_slice_in_dim(
        approx, lax.axis_index("rep") * owned_rows, owned_rows, 0
    )
    moment_new = MOMENTUM * qkv_moment + update_rows
    master_new = qkv_master - LEARNING_RATE * moment_new
    weight_bf16 = lax.all_gather(master_new.astype(jnp.bfloat16), "rep", axis=0, tiled=True)
    word_new = word_update(word_grads, token_ids, owner_map, word_master)
    return (error_new, right_basis, moment_new, master_new, weight_bf16, word_new)


def solution(mesh):
    in_specs = (
        P(("rep", "tp"), None),
        P("rep", "tp"),
        P("rep", None, "tp"),
        P("tp", None),
        P("rep", "tp"),
        P("rep", "tp"),
        P("rep", "tp"),
        P("rep"),
        P(),
        P("rep", "tp"),
    )
    out_specs = (
        P("rep", None, "tp"),
        P("tp", None),
        P("rep", "tp"),
        P("rep", "tp"),
        P(None, "tp"),
        P("rep", "tp"),
    )
    return jax.shard_map(shards, mesh=mesh, in_specs=in_specs, out_specs=out_specs, check_vma=False)
```

```python
import jax
import jax.numpy as jnp
from jax import lax
from jax.sharding import PartitionSpec as P

ROUNDS = 2


MOMENTUM = 0.9
LEARNING_RATE = 4.0
EMBED_RATE = 0.5


def tree_sum(value, axes):
    if isinstance(axes, str):
        axes = (axes,)
    count = 1
    for axis in axes:
        count *= lax.axis_size(axis)
    if count & (count - 1):
        return lax.psum(value, axes)
    def exchange(stride):
        return lax.ppermute(value, axes, [(i, i ^ stride) for i in range(count)])

    stride = 1
    if (count.bit_length() - 1) % 2:
        value = value + exchange(1)
        stride = 2
    while stride < count:
        low, high = stride, 2 * stride
        value = (value + exchange(low)) + (exchange(high) + exchange(low ^ high))
        stride *= 4
    return value


def replica_product(block, out_grads, axis):
    count = lax.axis_size(axis)
    if count != 8 or block.shape[0] % 2:
        gathered = lax.all_gather(block, axis, axis=0, tiled=True)
        return lax.dot_general(
            gathered, out_grads, (((0,), (0,)), ((), ())), preferred_element_type=jnp.float32
        )
    me = lax.axis_index(axis)

    def exchange(value, stride):
        return lax.ppermute(value, axis, [(i, i ^ stride) for i in range(count)])

    from_x = exchange(block, 2)
    from_y = exchange(block, 4)
    half = block.shape[0] // 2
    diagonal = jnp.concatenate(
        [exchange(from_y[:half], 2), exchange(from_x[half:], 4)], axis=0
    )
    mine = jnp.stack([block, from_x, from_y, diagonal])
    other = exchange(mine, 1)
    rows = block.shape[0]
    grads = out_grads.reshape(count, rows, out_grads.shape[1])
    even = jnp.stack([grads[me ^ offset] for offset in (0, 2, 4, 6)])
    odd = jnp.stack([grads[me ^ offset] for offset in (1, 3, 5, 7)])
    contract = (((0, 1), (0, 1)), ((), ()))
    first = lax.dot_general(mine, even, contract, preferred_element_type=jnp.float32)
    return first, (other, odd)


def split_tree_sum(value, axes):
    count = 1
    for axis in axes:
        count *= lax.axis_size(axis)
    rows = value.shape[0]
    if count & (count - 1) or count < 4 or rows % 2:
        return tree_sum(value, axes)

    def exchange(piece, stride):
        return lax.ppermute(piece, axes, [(i, i ^ stride) for i in range(count)])

    half = rows // 2
    core = lax.axis_index(axes[-1]) % 2
    kept = lax.dynamic_slice_in_dim(value, core * half, half, 0)
    given = lax.dynamic_slice_in_dim(value, (1 - core) * half, half, 0)
    kept = kept + exchange(given, 1)
    stride = 2
    while 4 * stride <= count:
        low, high = stride, 2 * stride
        kept = (kept + exchange(kept, low)) + (exchange(kept, high) + exchange(kept, low ^ high))
        stride *= 4
    while stride < count:
        kept = kept + exchange(kept, stride)
        stride *= 2
    other = exchange(kept, 1)
    total = jnp.zeros(value.shape, value.dtype)
    total = lax.dynamic_update_slice_in_dim(total, kept, core * half, 0)
    return lax.dynamic_update_slice_in_dim(total, other, (1 - core) * half, 0)


def orthonormal(left_basis, gram_matrix):
    factor_low = jnp.linalg.cholesky(gram_matrix)
    return jax.scipy.linalg.solve_triangular(factor_low, left_basis.T, lower=True).T


def word_update_dense(word_grads, token_ids, owner_map, word_master):
    replicas = lax.axis_size("rep")
    per_owner = word_master.shape[0]
    vocab = owner_map.shape[0]
    hits = token_ids[:, None] == jnp.arange(vocab, dtype=jnp.int32)[None, :]
    targets = jnp.sum(jnp.where(hits, owner_map[None, :], 0), axis=1)
    selector = (
        targets[:, None] == jnp.arange(replicas * per_owner, dtype=jnp.int32)[None, :]
    ).astype(jnp.bfloat16)
    partial = lax.dot_general(
        selector, word_grads, (((0,), (0,)), ((), ())), preferred_element_type=jnp.float32
    )
    me = lax.axis_index("rep")
    blocks = partial.reshape(replicas, per_owner, partial.shape[1])
    stride = 1
    while stride < replicas:
        bit = (me // stride) % 2
        paired = blocks.reshape((replicas // (2 * stride), 2) + blocks.shape[1:])
        kept = lax.dynamic_index_in_dim(paired, bit, axis=1, keepdims=False)
        sent = lax.dynamic_index_in_dim(paired, 1 - bit, axis=1, keepdims=False)
        pairs = [(i, i ^ stride) for i in range(replicas)]
        blocks = kept + lax.ppermute(sent, "rep", pairs)
        stride *= 2
    row_grad = blocks[0]
    return word_master - EMBED_RATE * row_grad


def word_update(word_grads, token_ids, owner_map, word_master):
    replicas = lax.axis_size("rep")
    if owner_map.shape[0] <= 4096 and replicas <= 8 and not replicas & (replicas - 1):
        return word_update_dense(word_grads, token_ids, owner_map, word_master)
    per_owner = word_master.shape[0]
    capacity = 2 * token_ids.shape[0] // replicas
    targets = owner_map[token_ids]
    owners = targets // per_owner
    row_slot = targets % per_owner
    matches = (owners[:, None] == jnp.arange(replicas, dtype=jnp.int32)[None, :]).astype(jnp.int32)
    places = jnp.sum(jnp.cumsum(matches, axis=0) * matches, axis=1) - 1
    outgoing = (
        jnp.zeros((replicas, capacity, word_grads.shape[1]), jnp.bfloat16)
        .at[owners, places]
        .set(word_grads)
    )
    labels = jnp.full((replicas, capacity), per_owner, jnp.int32).at[owners, places].set(row_slot)
    incoming, arrived = (
        lax.all_to_all(outgoing, "rep", split_axis=0, concat_axis=0, tiled=True),
        lax.all_to_all(labels, "rep", split_axis=0, concat_axis=0, tiled=True),
    )
    flat_rows = incoming.reshape(-1, incoming.shape[2])
    selector = (
        arrived.reshape(-1)[:, None] == jnp.arange(per_owner, dtype=jnp.int32)[None, :]
    ).astype(jnp.bfloat16)
    row_grad = lax.dot_general(
        selector, flat_rows, (((0,), (0,)), ((), ())), preferred_element_type=jnp.float32
    )
    return word_master - EMBED_RATE * row_grad


def shards(
    activations,
    out_grads,
    error_state,
    q_start,
    qkv_master,
    qkv_moment,
    word_grads,
    token_ids,
    owner_map,
    word_master,
):
    highest = lax.Precision.HIGHEST
    high = lax.Precision.HIGH
    replicas = lax.axis_size("rep")
    word_new = None
    early, late = replica_product(activations, out_grads, "tp")
    combined = early + error_state[0].astype(jnp.float32)
    right_rows = q_start.T
    left_rows = None
    for round_index in range(ROUNDS):
        partial_left = lax.dot_general(
            right_rows, combined, (((1,), (1,)), ((), ())), precision=high
        )
        if late is not None:
            other, odd = late
            partial_left, other = lax.optimization_barrier((partial_left, other))
            contract = (((0, 1), (0, 1)), ((), ()))
            second = lax.dot_general(other, odd, contract, preferred_element_type=jnp.float32)
            partial_left = partial_left + lax.dot_general(
                right_rows, second, (((1,), (1,)), ((), ())), precision=high
            )
            combined = combined + second
            late = None
        left_rows = split_tree_sum(partial_left, ("rep", "tp")) / replicas
        gram_matrix = jnp.dot(left_rows, left_rows.T, precision=high)
        factor_low = lax.linalg.cholesky(gram_matrix, symmetrize_input=False)
        left_rows = jax.scipy.linalg.solve_triangular(factor_low, left_rows, lower=True)
        partial_right = jnp.dot(left_rows, combined, precision=high)
        right_rows = tree_sum(partial_right, "rep") / replicas
    right_basis = right_rows.T
    approx = lax.dot_general(
        left_rows, right_rows, (((0,), (0,)), ((), ())), precision=high
    )
    error_new = (combined - approx).astype(jnp.bfloat16)[None]
    owned_rows = qkv_master.shape[0]
    update_rows = lax.dynamic_slice_in_dim(
        approx, lax.axis_index("rep") * owned_rows, owned_rows, 0
    )
    moment_new = MOMENTUM * qkv_moment + update_rows
    master_new = qkv_master - LEARNING_RATE * moment_new
    weight_bf16 = lax.all_gather(master_new.astype(jnp.bfloat16), "rep", axis=0, tiled=True)
    word_new = word_update(word_grads, token_ids, owner_map, word_master)
    return (error_new, right_basis, moment_new, master_new, weight_bf16, word_new)


def solution(mesh):
    in_specs = (
        P(("rep", "tp"), None),
        P("rep", "tp"),
        P("rep", None, "tp"),
        P("tp", None),
        P("rep", "tp"),
        P("rep", "tp"),
        P("rep", "tp"),
        P("rep"),
        P(),
        P("rep", "tp"),
    )
    out_specs = (
        P("rep", None, "tp"),
        P("tp", None),
        P("rep", "tp"),
        P("rep", "tp"),
        P(None, "tp"),
        P("rep", "tp"),
    )
    return jax.shard_map(shards, mesh=mesh, in_specs=in_specs, out_specs=out_specs, check_vma=False)
```

```python
import jax
import jax.numpy as jnp
from jax import lax
from jax.sharding import PartitionSpec as P

ROUNDS = 2


MOMENTUM = 0.9
LEARNING_RATE = 4.0
EMBED_RATE = 0.5


def tree_sum(value, axes):
    if isinstance(axes, str):
        axes = (axes,)
    count = 1
    for axis in axes:
        count *= lax.axis_size(axis)
    if count & (count - 1):
        return lax.psum(value, axes)
    def exchange(stride):
        return lax.ppermute(value, axes, [(i, i ^ stride) for i in range(count)])

    stride = 1
    if (count.bit_length() - 1) % 2:
        value = value + exchange(1)
        stride = 2
    while stride < count:
        low, high = stride, 2 * stride
        value = (value + exchange(low)) + (exchange(high) + exchange(low ^ high))
        stride *= 4
    return value


def replica_product(block, out_grads, axis):
    count = lax.axis_size(axis)
    if count != 8 or block.shape[0] % 2:
        gathered = lax.all_gather(block, axis, axis=0, tiled=True)
        return lax.dot_general(
            gathered, out_grads, (((0,), (0,)), ((), ())), preferred_element_type=jnp.float32
        )
    me = lax.axis_index(axis)

    def exchange(value, stride):
        return lax.ppermute(value, axis, [(i, i ^ stride) for i in range(count)])

    from_x = exchange(block, 2)
    from_y = exchange(block, 4)
    partner = exchange(block, 1)
    half = block.shape[0] // 2
    diagonal = jnp.concatenate(
        [exchange(from_y[:half], 2), exchange(from_x[half:], 4)], axis=0
    )
    mine = jnp.stack([block, from_x, from_y, diagonal])
    other = exchange(jnp.stack([from_x, from_y, diagonal]), 1)
    rows = block.shape[0]
    grads = out_grads.reshape(count, rows, out_grads.shape[1])
    even = jnp.stack([grads[me ^ offset] for offset in (0, 2, 4, 6)])
    odd = jnp.stack([grads[me ^ offset] for offset in (3, 5, 7)])
    contract = (((0, 1), (0, 1)), ((), ()))
    first = lax.dot_general(mine, even, contract, preferred_element_type=jnp.float32)
    first = first + lax.dot_general(
        partner, grads[me ^ 1], (((0,), (0,)), ((), ())), preferred_element_type=jnp.float32
    )
    return first, (other, odd)


def split_tree_sum(value, axes):
    count = 1
    for axis in axes:
        count *= lax.axis_size(axis)
    rows = value.shape[0]
    if count & (count - 1) or count < 4 or rows % 2:
        return tree_sum(value, axes)

    def exchange(piece, stride):
        return lax.ppermute(piece, axes, [(i, i ^ stride) for i in range(count)])

    half = rows // 2
    core = lax.axis_index(axes[-1]) % 2
    kept = lax.dynamic_slice_in_dim(value, core * half, half, 0)
    given = lax.dynamic_slice_in_dim(value, (1 - core) * half, half, 0)
    kept = kept + exchange(given, 1)
    stride = 2
    while 4 * stride <= count:
        low, high = stride, 2 * stride
        kept = (kept + exchange(kept, low)) + (exchange(kept, high) + exchange(kept, low ^ high))
        stride *= 4
    while stride < count:
        kept = kept + exchange(kept, stride)
        stride *= 2
    other = exchange(kept, 1)
    total = jnp.zeros(value.shape, value.dtype)
    total = lax.dynamic_update_slice_in_dim(total, kept, core * half, 0)
    return lax.dynamic_update_slice_in_dim(total, other, (1 - core) * half, 0)


def orthonormal(left_basis, gram_matrix):
    factor_low = jnp.linalg.cholesky(gram_matrix)
    return jax.scipy.linalg.solve_triangular(factor_low, left_basis.T, lower=True).T


def word_update_dense(word_grads, token_ids, owner_map, word_master):
    replicas = lax.axis_size("rep")
    per_owner = word_master.shape[0]
    vocab = owner_map.shape[0]
    hits = token_ids[:, None] == jnp.arange(vocab, dtype=jnp.int32)[None, :]
    targets = jnp.sum(jnp.where(hits, owner_map[None, :], 0), axis=1)
    selector = (
        targets[:, None] == jnp.arange(replicas * per_owner, dtype=jnp.int32)[None, :]
    ).astype(jnp.bfloat16)
    partial = lax.dot_general(
        selector, word_grads, (((0,), (0,)), ((), ())), preferred_element_type=jnp.float32
    )
    me = lax.axis_index("rep")
    blocks = partial.reshape(replicas, per_owner, partial.shape[1])
    stride = 1
    while stride < replicas:
        bit = (me // stride) % 2
        paired = blocks.reshape((replicas // (2 * stride), 2) + blocks.shape[1:])
        kept = lax.dynamic_index_in_dim(paired, bit, axis=1, keepdims=False)
        sent = lax.dynamic_index_in_dim(paired, 1 - bit, axis=1, keepdims=False)
        pairs = [(i, i ^ stride) for i in range(replicas)]
        blocks = kept + lax.ppermute(sent, "rep", pairs)
        stride *= 2
    row_grad = blocks[0]
    return word_master - EMBED_RATE * row_grad


def word_update(word_grads, token_ids, owner_map, word_master):
    replicas = lax.axis_size("rep")
    if owner_map.shape[0] <= 4096 and replicas <= 8 and not replicas & (replicas - 1):
        return word_update_dense(word_grads, token_ids, owner_map, word_master)
    per_owner = word_master.shape[0]
    capacity = 2 * token_ids.shape[0] // replicas
    targets = owner_map[token_ids]
    owners = targets // per_owner
    row_slot = targets % per_owner
    matches = (owners[:, None] == jnp.arange(replicas, dtype=jnp.int32)[None, :]).astype(jnp.int32)
    places = jnp.sum(jnp.cumsum(matches, axis=0) * matches, axis=1) - 1
    outgoing = (
        jnp.zeros((replicas, capacity, word_grads.shape[1]), jnp.bfloat16)
        .at[owners, places]
        .set(word_grads)
    )
    labels = jnp.full((replicas, capacity), per_owner, jnp.int32).at[owners, places].set(row_slot)
    incoming, arrived = (
        lax.all_to_all(outgoing, "rep", split_axis=0, concat_axis=0, tiled=True),
        lax.all_to_all(labels, "rep", split_axis=0, concat_axis=0, tiled=True),
    )
    flat_rows = incoming.reshape(-1, incoming.shape[2])
    selector = (
        arrived.reshape(-1)[:, None] == jnp.arange(per_owner, dtype=jnp.int32)[None, :]
    ).astype(jnp.bfloat16)
    row_grad = lax.dot_general(
        selector, flat_rows, (((0,), (0,)), ((), ())), preferred_element_type=jnp.float32
    )
    return word_master - EMBED_RATE * row_grad


def shards(
    activations,
    out_grads,
    error_state,
    q_start,
    qkv_master,
    qkv_moment,
    word_grads,
    token_ids,
    owner_map,
    word_master,
):
    highest = lax.Precision.HIGHEST
    high = lax.Precision.HIGH
    replicas = lax.axis_size("rep")
    word_new = None
    early, late = replica_product(activations, out_grads, "tp")
    combined = early + error_state[0].astype(jnp.float32)
    right_rows = q_start.T
    left_rows = None
    for round_index in range(ROUNDS):
        partial_left = lax.dot_general(
            right_rows, combined, (((1,), (1,)), ((), ())), precision=high
        )
        if late is not None:
            other, odd = late
            partial_left, other = lax.optimization_barrier((partial_left, other))
            contract = (((0, 1), (0, 1)), ((), ()))
            second = lax.dot_general(other, odd, contract, preferred_element_type=jnp.float32)
            partial_left = partial_left + lax.dot_general(
                right_rows, second, (((1,), (1,)), ((), ())), precision=high
            )
            combined = combined + second
            late = None
        left_rows = split_tree_sum(partial_left, ("rep", "tp")) / replicas
        gram_matrix = jnp.dot(left_rows, left_rows.T, precision=high)
        factor_low = lax.linalg.cholesky(gram_matrix, symmetrize_input=False)
        left_rows = jax.scipy.linalg.solve_triangular(factor_low, left_rows, lower=True)
        partial_right = jnp.dot(left_rows, combined, precision=high)
        right_rows = tree_sum(partial_right, "rep") / replicas
    right_basis = right_rows.T
    approx = lax.dot_general(
        left_rows, right_rows, (((0,), (0,)), ((), ())), precision=high
    )
    error_new = (combined - approx).astype(jnp.bfloat16)[None]
    owned_rows = qkv_master.shape[0]
    update_rows = lax.dynamic_slice_in_dim(
        approx, lax.axis_index("rep") * owned_rows, owned_rows, 0
    )
    moment_new = MOMENTUM * qkv_moment + update_rows
    master_new = qkv_master - LEARNING_RATE * moment_new
    weight_bf16 = lax.all_gather(master_new.astype(jnp.bfloat16), "rep", axis=0, tiled=True)
    word_new = word_update(word_grads, token_ids, owner_map, word_master)
    return (error_new, right_basis, moment_new, master_new, weight_bf16, word_new)


def solution(mesh):
    in_specs = (
        P(("rep", "tp"), None),
        P("rep", "tp"),
        P("rep", None, "tp"),
        P("tp", None),
        P("rep", "tp"),
        P("rep", "tp"),
        P("rep", "tp"),
        P("rep"),
        P(),
        P("rep", "tp"),
    )
    out_specs = (
        P("rep", None, "tp"),
        P("tp", None),
        P("rep", "tp"),
        P("rep", "tp"),
        P(None, "tp"),
        P("rep", "tp"),
    )
    return jax.shard_map(shards, mesh=mesh, in_specs=in_specs, out_specs=out_specs, check_vma=False)
```

```python
import jax
import jax.numpy as jnp
from jax import lax
from jax.sharding import PartitionSpec as P

ROUNDS = 2


MOMENTUM = 0.9
LEARNING_RATE = 4.0
EMBED_RATE = 0.5


def tree_sum(value, axes):
    if isinstance(axes, str):
        axes = (axes,)
    count = 1
    for axis in axes:
        count *= lax.axis_size(axis)
    if count & (count - 1):
        return lax.psum(value, axes)
    def exchange(stride):
        return lax.ppermute(value, axes, [(i, i ^ stride) for i in range(count)])

    stride = 1
    if (count.bit_length() - 1) % 2:
        value = value + exchange(1)
        stride = 2
    while stride < count:
        low, high = stride, 2 * stride
        value = (value + exchange(low)) + (exchange(high) + exchange(low ^ high))
        stride *= 4
    return value


def replica_product(block, out_grads, axis):
    count = lax.axis_size(axis)
    if count != 8 or block.shape[0] % 2:
        gathered = lax.all_gather(block, axis, axis=0, tiled=True)
        return lax.dot_general(
            gathered, out_grads, (((0,), (0,)), ((), ())), preferred_element_type=jnp.float32
        )
    me = lax.axis_index(axis)

    def exchange(value, stride):
        return lax.ppermute(value, axis, [(i, i ^ stride) for i in range(count)])

    from_x = exchange(block, 2)
    from_y = exchange(block, 4)
    half = block.shape[0] // 2
    diagonal = jnp.concatenate(
        [exchange(from_y[:half], 2), exchange(from_x[half:], 4)], axis=0
    )
    mine = jnp.stack([block, from_x, from_y, diagonal])
    other = exchange(mine, 1)
    rows = block.shape[0]
    grads = out_grads.reshape(count, rows, out_grads.shape[1])
    even = jnp.stack([grads[me ^ offset] for offset in (0, 2, 4, 6)])
    odd = jnp.stack([grads[me ^ offset] for offset in (1, 3, 5, 7)])
    contract = (((0, 1), (0, 1)), ((), ()))
    first = lax.dot_general(mine, even, contract, preferred_element_type=jnp.float32)
    return first, (other, odd)


def split_tree_sum(value, axes):
    count = 1
    for axis in axes:
        count *= lax.axis_size(axis)
    rows = value.shape[0]
    if count & (count - 1) or count < 4 or rows % 2:
        return tree_sum(value, axes)

    def exchange(piece, stride):
        return lax.ppermute(piece, axes, [(i, i ^ stride) for i in range(count)])

    half = rows // 2
    core = lax.axis_index(axes[-1]) % 2
    kept = lax.dynamic_slice_in_dim(value, core * half, half, 0)
    given = lax.dynamic_slice_in_dim(value, (1 - core) * half, half, 0)
    kept = kept + exchange(given, 1)
    stride = 2
    while 4 * stride <= count:
        low, high = stride, 2 * stride
        kept = (kept + exchange(kept, low)) + (exchange(kept, high) + exchange(kept, low ^ high))
        stride *= 4
    while stride < count:
        kept = kept + exchange(kept, stride)
        stride *= 2
    other = exchange(kept, 1)
    low_first = jnp.concatenate([kept, other], axis=0)
    high_first = jnp.concatenate([other, kept], axis=0)
    return jnp.where(core == 0, low_first, high_first)


def orthonormal(left_basis, gram_matrix):
    factor_low = jnp.linalg.cholesky(gram_matrix)
    return jax.scipy.linalg.solve_triangular(factor_low, left_basis.T, lower=True).T


def word_update_dense(word_grads, token_ids, owner_map, word_master):
    replicas = lax.axis_size("rep")
    per_owner = word_master.shape[0]
    vocab = owner_map.shape[0]
    hits = token_ids[:, None] == jnp.arange(vocab, dtype=jnp.int32)[None, :]
    targets = jnp.sum(jnp.where(hits, owner_map[None, :], 0), axis=1)
    selector = (
        targets[:, None] == jnp.arange(replicas * per_owner, dtype=jnp.int32)[None, :]
    ).astype(jnp.bfloat16)
    partial = lax.dot_general(
        selector, word_grads, (((0,), (0,)), ((), ())), preferred_element_type=jnp.float32
    )
    me = lax.axis_index("rep")
    blocks = partial.reshape(replicas, per_owner, partial.shape[1])
    stride = 1
    while stride < replicas:
        bit = (me // stride) % 2
        paired = blocks.reshape((replicas // (2 * stride), 2) + blocks.shape[1:])
        kept = lax.dynamic_index_in_dim(paired, bit, axis=1, keepdims=False)
        sent = lax.dynamic_index_in_dim(paired, 1 - bit, axis=1, keepdims=False)
        pairs = [(i, i ^ stride) for i in range(replicas)]
        blocks = kept + lax.ppermute(sent, "rep", pairs)
        stride *= 2
    row_grad = blocks[0]
    return word_master - EMBED_RATE * row_grad


def word_update(word_grads, token_ids, owner_map, word_master):
    replicas = lax.axis_size("rep")
    if owner_map.shape[0] <= 4096 and replicas <= 8 and not replicas & (replicas - 1):
        return word_update_dense(word_grads, token_ids, owner_map, word_master)
    per_owner = word_master.shape[0]
    capacity = 2 * token_ids.shape[0] // replicas
    targets = owner_map[token_ids]
    owners = targets // per_owner
    row_slot = targets % per_owner
    matches = (owners[:, None] == jnp.arange(replicas, dtype=jnp.int32)[None, :]).astype(jnp.int32)
    places = jnp.sum(jnp.cumsum(matches, axis=0) * matches, axis=1) - 1
    outgoing = (
        jnp.zeros((replicas, capacity, word_grads.shape[1]), jnp.bfloat16)
        .at[owners, places]
        .set(word_grads)
    )
    labels = jnp.full((replicas, capacity), per_owner, jnp.int32).at[owners, places].set(row_slot)
    incoming, arrived = (
        lax.all_to_all(outgoing, "rep", split_axis=0, concat_axis=0, tiled=True),
        lax.all_to_all(labels, "rep", split_axis=0, concat_axis=0, tiled=True),
    )
    flat_rows = incoming.reshape(-1, incoming.shape[2])
    selector = (
        arrived.reshape(-1)[:, None] == jnp.arange(per_owner, dtype=jnp.int32)[None, :]
    ).astype(jnp.bfloat16)
    row_grad = lax.dot_general(
        selector, flat_rows, (((0,), (0,)), ((), ())), preferred_element_type=jnp.float32
    )
    return word_master - EMBED_RATE * row_grad


def shards(
    activations,
    out_grads,
    error_state,
    q_start,
    qkv_master,
    qkv_moment,
    word_grads,
    token_ids,
    owner_map,
    word_master,
):
    highest = lax.Precision.HIGHEST
    high = lax.Precision.HIGH
    replicas = lax.axis_size("rep")
    word_new = None
    early, late = replica_product(activations, out_grads, "tp")
    combined = early + error_state[0].astype(jnp.float32)
    right_rows = q_start.T
    left_rows = None
    for round_index in range(ROUNDS):
        partial_left = lax.dot_general(
            right_rows, combined, (((1,), (1,)), ((), ())), precision=high
        )
        if late is not None:
            other, odd = late
            partial_left, other = lax.optimization_barrier((partial_left, other))
            contract = (((0, 1), (0, 1)), ((), ()))
            second = lax.dot_general(other, odd, contract, preferred_element_type=jnp.float32)
            partial_left = partial_left + lax.dot_general(
                right_rows, second, (((1,), (1,)), ((), ())), precision=high
            )
            combined = combined + second
            late = None
        left_rows = split_tree_sum(partial_left, ("rep", "tp")) / replicas
        gram_matrix = jnp.dot(left_rows, left_rows.T, precision=high)
        factor_low = lax.linalg.cholesky(gram_matrix, symmetrize_input=False)
        left_rows = jax.scipy.linalg.solve_triangular(factor_low, left_rows, lower=True)
        partial_right = jnp.dot(left_rows, combined, precision=high)
        right_rows = tree_sum(partial_right, "rep") / replicas
    right_basis = right_rows.T
    approx = lax.dot_general(
        left_rows, right_rows, (((0,), (0,)), ((), ())), precision=high
    )
    error_new = (combined - approx).astype(jnp.bfloat16)[None]
    owned_rows = qkv_master.shape[0]
    update_rows = lax.dynamic_slice_in_dim(
        approx, lax.axis_index("rep") * owned_rows, owned_rows, 0
    )
    moment_new = MOMENTUM * qkv_moment + update_rows
    master_new = qkv_master - LEARNING_RATE * moment_new
    weight_bf16 = lax.all_gather(master_new.astype(jnp.bfloat16), "rep", axis=0, tiled=True)
    word_new = word_update(word_grads, token_ids, owner_map, word_master)
    return (error_new, right_basis, moment_new, master_new, weight_bf16, word_new)


def solution(mesh):
    in_specs = (
        P(("rep", "tp"), None),
        P("rep", "tp"),
        P("rep", None, "tp"),
        P("tp", None),
        P("rep", "tp"),
        P("rep", "tp"),
        P("rep", "tp"),
        P("rep"),
        P(),
        P("rep", "tp"),
    )
    out_specs = (
        P("rep", None, "tp"),
        P("tp", None),
        P("rep", "tp"),
        P("rep", "tp"),
        P(None, "tp"),
        P("rep", "tp"),
    )
    return jax.shard_map(shards, mesh=mesh, in_specs=in_specs, out_specs=out_specs, check_vma=False)
```
